128 devices in a mesh: tok: 8 (over z, core), wid: 16 (over y, x).
Axes of the slice: x: 4, y: 4, z: 4, core: 2. Of those that a mesh axis runs over, the one named last changes fastest.
Arguments:
- tokens: bfloat16 [8192, 3072], P('tok', 'wid'), may hold values from -6 to 6
- defect_mask: int32 [8192], P('tok'), may hold values 0 or 1
- timestep: int32 [1], replicated, may hold values from 0 to 999
- mask_embed: bfloat16 [3072], P('wid'), may hold values from -6 to 6
- mod_weight: bfloat16 [256, 3, 3072], P(None, None, 'wid'), may hold values from -0.375 to 0.375
- w_qkv: bfloat16 [3072, 3, 2048], P('tok', None, 'wid'), may hold values from -1.4614179 to 1.4614179, as said below
- w_out: bfloat16 [2048, 3072], P('wid'), may hold values from -0.125 to 0.125
Outputs:
- block_out: bfloat16 [8192, 3072], P('tok', 'wid')
The draws below stay inside these ranges and needn't reach their ends.
Inputs may be any that keep to these rules, and one draw needn't show every extreme that they name: `w_qkv`: entries are at most 81 / sqrt(3072) in magnitude.
All inputs are finite; a program needn't handle non-finite values. No bound on the sum of `defect_mask` on one device may be relied on, other than what follows from the above.
Results may differ from the reference program's by a relative error of at most 0.011.
Values may be sent and summed in bfloat16 or wider, within the bound.
No kernel may reach another device: no remote copies, remote signals or barrier semaphores. Data moves between devices by JAX's collectives and lax.ppermute only.
A program may use at most 128 MiB of HBM per device.

```python
import math
import jax
import jax.numpy as jnp
from jax import lax

D = 3072
H = 16
DH = 128
TEMB = 256
TOKENS = 8192
HD = 2048


def draw_w_qkv(key, part):
    base = jax.random.truncated_normal(key, -4.0, 4.0, (D, 3, H * DH), jnp.float32)
    gains = jnp.array([2.0, 2.0, 1.0], jnp.float32)[None, :, None] * D ** (-0.5)
    weight = base * gains
    return weight.astype(jnp.bfloat16)


def set_ends(values, rng, least, largest):
    shape = values.shape
    spot = [jax.random.randint(jax.random.fold_in(rng, axis), (), 0, shape[axis]) for axis in range(len(shape))]
    values = values.at[tuple(spot)].set(least)
    longest = shape.index(max(shape))
    spot[longest] = (spot[longest] + 1) % shape[longest]
    return values.at[tuple(spot)].set(largest)


def block_scale(key, dims, shards, low, high):
    loudness, own = 1.0, jax.random.fold_in(key, 6)
    for dim, blocks in shards:
        draws = jnp.exp(jax.random.uniform(jax.random.fold_in(own, dim), (blocks,), jnp.float32, low / len(shards), high / len(shards)))
        loudness = loudness * jnp.repeat(draws, dims[dim] // blocks).reshape([-1 if axis == dim else 1 for axis in range(len(dims))])
    return loudness


def bell_draw(rng, extent, scale, limit, pieces=(), held_as=jnp.bfloat16):
    gain = block_scale(rng, extent, pieces, -0.22, 0.18) if pieces else 1.0
    result = jax.random.normal(rng, extent, jnp.float32) * scale * gain
    return jnp.minimum(jnp.maximum(result, -limit), limit).astype(held_as)


def setup_inputs(seed: int = 0) -> dict:
    seeds = jax.random.split(jax.random.key(seed), 8)
    tokens = bell_draw(seeds[0], (TOKENS, D), 1.0, 6.0, ((0, 8), (1, 16)))
    defect_mask = set_ends((jax.random.randint(seeds[1], (TOKENS,), 0, 2) < 1).astype(jnp.int32), jax.random.fold_in(seeds[1], 1), 0, 1)
    timestep = jax.random.randint(seeds[2], (1,), 0, 1000).astype(jnp.int32)
    mask_embed = bell_draw(seeds[3], (D,), 1.0, 6.0, ((0, 16),))
    mod_weight = bell_draw(seeds[4], (TEMB, 3, D), TEMB ** -0.5, 0.375, ((2, 16),))
    w_qkv = draw_w_qkv(jax.random.fold_in(seeds[7], 71), 0)
    w_out = bell_draw(seeds[6], (HD, D), HD ** -0.5, 0.125, ((0, 16),))
    return dict(tokens=tokens, defect_mask=defect_mask, timestep=timestep, mask_embed=mask_embed, mod_weight=mod_weight, w_qkv=w_qkv, w_out=w_out)


def modulate_rows(rows, shift_row, scale_row):
    values = rows.astype(jnp.float32)
    row_mean = lax.optimization_barrier(jnp.mean(values, axis=1, keepdims=True))
    row_var = lax.optimization_barrier(jnp.mean(values * values, axis=1, keepdims=True)) - row_mean * row_mean
    normal = (values - row_mean) * lax.rsqrt(row_var + 1e-06)
    return (normal * (1.0 + scale_row.astype(jnp.float32)) + shift_row.astype(jnp.float32)).astype(jnp.bfloat16)

def reference(tokens, defect_mask, timestep, mask_embed, mod_weight, w_qkv, w_out):
    residual_in = (tokens.astype(jnp.float32) + defect_mask.astype(jnp.float32)[:, None] * mask_embed.astype(jnp.float32)[None, :]).astype(jnp.bfloat16)
    half_width = TEMB // 2
    frequency = jnp.exp(-math.log(10000.0) * jnp.arange(half_width, dtype=jnp.float32) / half_width)
    angles = timestep.astype(jnp.float32)[0] * frequency
    embedding = jnp.concatenate([jnp.cos(angles), jnp.sin(angles)])
    modulation = jnp.einsum('e,ecf->cf', jax.nn.silu(embedding), mod_weight.astype(jnp.float32), precision=lax.Precision.HIGHEST).astype(jnp.bfloat16)
    normed = modulate_rows(residual_in, modulation[0][None, :], modulation[1][None, :])
    qkv = jnp.dot(normed, w_qkv.reshape(D, 3 * H * DH), preferred_element_type=jnp.float32).astype(jnp.bfloat16)
    qkv = qkv.reshape(TOKENS, 3, H, DH)
    queries = jnp.transpose(qkv[:, 0], (1, 0, 2))
    keys_all = jnp.transpose(qkv[:, 1], (1, 0, 2))
    values_all = jnp.transpose(qkv[:, 2], (1, 0, 2))

    def one_head(operands):
        query_head, key_head, value_head = operands
        scores = jnp.dot(query_head, key_head.T, preferred_element_type=jnp.float32) * DH ** (-0.5)
        shifted = jnp.exp(scores - lax.optimization_barrier(jnp.max(scores, axis=1, keepdims=True)))
        weights = shifted.astype(jnp.bfloat16)
        numer = jnp.dot(weights, value_head, preferred_element_type=jnp.float32)
        return numer / lax.optimization_barrier(jnp.sum(shifted, axis=1, keepdims=True))
    attended = lax.map(one_head, (queries, keys_all, values_all))
    attended = jnp.transpose(attended, (1, 0, 2)).reshape(TOKENS, H * DH).astype(jnp.bfloat16)
    projected = jnp.dot(attended, w_out, preferred_element_type=jnp.float32)
    return (residual_in.astype(jnp.float32) + modulation[2].astype(jnp.float32)[None, :] * projected).astype(jnp.bfloat16)
```

```python
import math

import jax
import jax.numpy as jnp
from jax import lax
from jax.sharding import PartitionSpec as P

D = 3072
DH = 128
TEMB = 256


def finish_rows(values, row_mean, row_var, shift_row, scale_row):
    normal = (values - row_mean) * lax.rsqrt(row_var + 1e-06)
    return (normal * (1.0 + scale_row.astype(jnp.float32)) + shift_row.astype(jnp.float32)).astype(
        jnp.bfloat16
    )


def body(tokens, defect_mask, timestep, mask_embed, mod_weight, w_qkv, w_out):
    tok_rows = tokens.shape[0]
    residual_in = (
        tokens.astype(jnp.float32)
        + defect_mask.astype(jnp.float32)[:, None] * mask_embed.astype(jnp.float32)[None, :]
    ).astype(jnp.bfloat16)
    w_cols = lax.all_to_all(w_out, "wid", split_axis=1, concat_axis=0, tiled=True)
    w_full = lax.all_gather(w_qkv, "tok", axis=0, tiled=True)
    residual_full = lax.all_gather(residual_in, "wid", axis=1, tiled=True)
    half_width = TEMB // 2
    frequency = jnp.exp(-math.log(10000.0) * jnp.arange(half_width, dtype=jnp.float32) / half_width)
    angles = timestep.astype(jnp.float32)[0] * frequency
    embedding = jnp.concatenate([jnp.cos(angles), jnp.sin(angles)])
    modulation = jnp.einsum(
        "e,ecf->cf",
        jax.nn.silu(embedding),
        mod_weight.astype(jnp.float32),
        precision=lax.Precision.HIGHEST,
    ).astype(jnp.bfloat16)
    shift_scale = lax.all_gather(modulation[:2], "wid", axis=1, tiled=True)
    values = residual_full.astype(jnp.float32)
    row_mean = jnp.mean(values, axis=1, keepdims=True)
    row_var = jnp.mean(values * values, axis=1, keepdims=True) - row_mean * row_mean
    normed = finish_rows(values, row_mean, row_var, shift_scale[0][None, :], shift_scale[1][None, :])
    qkv = jnp.einsum(
        "td,dcf->tcf",
        normed,
        w_full,
        preferred_element_type=jnp.float32,
    ).astype(jnp.bfloat16)
    queries = qkv[:, 0]
    key_values = lax.all_gather(qkv[:, 1:3], "tok", axis=0, tiled=True)
    key_part = key_values[:, 0]
    value_part = key_values[:, 1]
    score_scale = DH ** (-0.5)
    scores = jnp.dot(queries, key_part.T, preferred_element_type=jnp.float32) * score_scale
    shifted = jnp.exp(scores - jnp.max(scores, axis=1, keepdims=True))
    row_sum = jnp.sum(shifted, axis=1, keepdims=True)
    numer = jnp.dot(shifted.astype(jnp.bfloat16), value_part, preferred_element_type=jnp.float32)
    attended = (numer / row_sum).astype(jnp.bfloat16)
    attended_full = lax.all_gather(attended, "wid", axis=1, tiled=True)
    projected = jnp.dot(attended_full, w_cols, preferred_element_type=jnp.float32)
    return (
        residual_in.astype(jnp.float32) + modulation[2].astype(jnp.float32)[None, :] * projected
    ).astype(jnp.bfloat16)


def solution(mesh):
    return jax.shard_map(
        body,
        mesh=mesh,
        in_specs=(
            P("tok", "wid"),
            P("tok"),
            P(),
            P("wid"),
            P(None, None, "wid"),
            P("tok", None, "wid"),
            P("wid", None),
        ),
        out_specs=P("tok", "wid"),
        check_vma=False,
    )
```

```python
import math

import jax
import jax.numpy as jnp
from jax import lax
from jax.sharding import PartitionSpec as P

D = 3072
DH = 128
TEMB = 256


def finish_rows(values, row_mean, row_var, shift_row, scale_row):
    normal = (values - row_mean) * lax.rsqrt(row_var + 1e-06)
    return (normal * (1.0 + scale_row.astype(jnp.float32)) + shift_row.astype(jnp.float32)).astype(
        jnp.bfloat16
    )


def body(tokens, defect_mask, timestep, mask_embed, mod_weight, w_qkv, w_out):
    tok_rows = tokens.shape[0]
    residual_in = (
        tokens.astype(jnp.float32)
        + defect_mask.astype(jnp.float32)[:, None] * mask_embed.astype(jnp.float32)[None, :]
    ).astype(jnp.bfloat16)
    w_cols = lax.all_to_all(w_out, "wid", split_axis=1, concat_axis=0, tiled=True)
    tok_count = lax.axis_size("tok")
    w_copies = jnp.broadcast_to(w_qkv[None], (tok_count,) + w_qkv.shape)
    w_full = lax.all_to_all(w_copies, "tok", split_axis=0, concat_axis=0, tiled=True)
    w_full = w_full.reshape((tok_count * w_qkv.shape[0],) + w_qkv.shape[1:])
    half_width = TEMB // 2
    frequency = jnp.exp(-math.log(10000.0) * jnp.arange(half_width, dtype=jnp.float32) / half_width)
    angles = timestep.astype(jnp.float32)[0] * frequency
    embedding = jnp.concatenate([jnp.cos(angles), jnp.sin(angles)])
    modulation = jnp.einsum(
        "e,ecf->cf",
        jax.nn.silu(embedding),
        mod_weight.astype(jnp.float32),
        precision=lax.Precision.HIGHEST,
    ).astype(jnp.bfloat16)
    extra = jnp.zeros((16, residual_in.shape[1]), jnp.bfloat16).at[:2].set(modulation[:2])
    packed = lax.all_gather(
        jnp.concatenate([residual_in, extra], axis=0), "wid", axis=1, tiled=True
    )
    residual_full = packed[:tok_rows]
    shift_scale = packed[tok_rows : tok_rows + 2]
    values = residual_full.astype(jnp.float32)
    row_mean = jnp.mean(values, axis=1, keepdims=True)
    row_var = jnp.mean(values * values, axis=1, keepdims=True) - row_mean * row_mean
    normed = finish_rows(values, row_mean, row_var, shift_scale[0][None, :], shift_scale[1][None, :])
    qkv = jnp.einsum(
        "td,dcf->tcf",
        normed,
        w_full,
        preferred_element_type=jnp.float32,
    ).astype(jnp.bfloat16)
    qkv, w_cols = lax.optimization_barrier((qkv, w_cols))
    queries = qkv[:, 0]
    key_values = lax.all_gather(qkv[:, 1:3], "tok", axis=0, tiled=True)
    key_part = key_values[:, 0]
    value_part = key_values[:, 1]
    score_scale = DH ** (-0.5)
    scores = jnp.dot(queries, key_part.T, preferred_element_type=jnp.float32) * score_scale
    shifted = jnp.exp(scores - jnp.max(scores, axis=1, keepdims=True))
    row_sum = jnp.sum(shifted, axis=1, keepdims=True)
    numer = jnp.dot(shifted.astype(jnp.bfloat16), value_part, preferred_element_type=jnp.float32)
    attended = (numer / row_sum).astype(jnp.bfloat16)
    attended_full = lax.all_gather(attended, "wid", axis=1, tiled=True)
    projected = jnp.dot(attended_full, w_cols, preferred_element_type=jnp.float32)
    return (
        residual_in.astype(jnp.float32) + modulation[2].astype(jnp.float32)[None, :] * projected
    ).astype(jnp.bfloat16)


def solution(mesh):
    return jax.shard_map(
        body,
        mesh=mesh,
        in_specs=(
            P("tok", "wid"),
            P("tok"),
            P(),
            P("wid"),
            P(None, None, "wid"),
            P("tok", None, "wid"),
            P("wid", None),
        ),
        out_specs=P("tok", "wid"),
        check_vma=False,
    )
```

```python
import math

import jax
import jax.numpy as jnp
from jax import lax
from jax.experimental import pallas as pl
from jax.experimental.pallas import tpu as pltpu
from jax.sharding import PartitionSpec as P

D = 3072
DH = 128
TEMB = 256


def finish_rows(values, row_mean, row_var, shift_row, scale_row):
    normal = (values - row_mean) * lax.rsqrt(row_var + 1e-06)
    return (normal * (1.0 + scale_row.astype(jnp.float32)) + shift_row.astype(jnp.float32)).astype(
        jnp.bfloat16
    )


def attention_kernel(q_ref, kv_ref, o_ref):
    keys = kv_ref[:, :DH]
    values = kv_ref[:, DH:]
    scores = lax.dot_general(
        q_ref[...], keys, (((1,), (1,)), ((), ())), preferred_element_type=jnp.float32
    ) * (DH ** (-0.5))
    shifted = jnp.exp(scores - jnp.max(scores, axis=1, keepdims=True))
    row_sum = jnp.sum(shifted, axis=1, keepdims=True)
    numer = jnp.dot(shifted.astype(jnp.bfloat16), values, preferred_element_type=jnp.float32)
    o_ref[...] = (numer / row_sum).astype(o_ref.dtype)


def attention(queries, key_values, block=256):
    rows = queries.shape[0]
    count = key_values.shape[0]
    return pl.pallas_call(
        attention_kernel,
        grid=(rows // block,),
        in_specs=[
            pl.BlockSpec((block, DH), lambda i: (i, 0)),
            pl.BlockSpec((count, 2 * DH), lambda i: (0, 0)),
        ],
        out_specs=pl.BlockSpec((block, DH), lambda i: (i, 0)),
        out_shape=jax.ShapeDtypeStruct((rows, DH), jnp.bfloat16),
        compiler_params=pltpu.CompilerParams(vmem_limit_bytes=56 * 1024 * 1024),
        cost_estimate=pl.CostEstimate(
            flops=4 * rows * count * DH,
            transcendentals=rows * count,
            bytes_accessed=4 * rows * DH + 4 * count * DH,
        ),
    )(queries, key_values)


def body(tokens, defect_mask, timestep, mask_embed, mod_weight, w_qkv, w_out):
    tok_rows = tokens.shape[0]
    residual_in = (
        tokens.astype(jnp.float32)
        + defect_mask.astype(jnp.float32)[:, None] * mask_embed.astype(jnp.float32)[None, :]
    ).astype(jnp.bfloat16)
    w_cols = lax.all_to_all(w_out, "wid", split_axis=1, concat_axis=0, tiled=True)
    tok_count = lax.axis_size("tok")
    w_copies = jnp.broadcast_to(w_qkv[None], (tok_count,) + w_qkv.shape)
    w_full = lax.all_to_all(w_copies, "tok", split_axis=0, concat_axis=0, tiled=True)
    w_full = w_full.reshape((tok_count * w_qkv.shape[0],) + w_qkv.shape[1:])
    half_width = TEMB // 2
    frequency = jnp.exp(-math.log(10000.0) * jnp.arange(half_width, dtype=jnp.float32) / half_width)
    angles = timestep.astype(jnp.float32)[0] * frequency
    embedding = jnp.concatenate([jnp.cos(angles), jnp.sin(angles)])
    modulation = jnp.einsum(
        "e,ecf->cf",
        jax.nn.silu(embedding),
        mod_weight.astype(jnp.float32),
        precision=lax.Precision.HIGHEST,
    ).astype(jnp.bfloat16)
    extra = jnp.zeros((16, residual_in.shape[1]), jnp.bfloat16).at[:2].set(modulation[:2])
    packed = lax.all_gather(
        jnp.concatenate([residual_in, extra], axis=0), "wid", axis=1, tiled=True
    )
    residual_full = packed[:tok_rows]
    shift_scale = packed[tok_rows : tok_rows + 2]
    values = residual_full.astype(jnp.float32)
    row_mean = jnp.mean(values, axis=1, keepdims=True)
    row_var = jnp.mean(values * values, axis=1, keepdims=True) - row_mean * row_mean
    normed = finish_rows(values, row_mean, row_var, shift_scale[0][None, :], shift_scale[1][None, :])
    qkv = jnp.einsum(
        "td,dcf->tcf",
        normed,
        w_full,
        preferred_element_type=jnp.float32,
    ).astype(jnp.bfloat16)
    qkv, w_cols = lax.optimization_barrier((qkv, w_cols))
    queries = qkv[:, 0]
    key_values = lax.all_gather(
        qkv[:, 1:3].reshape(tok_rows, 2 * DH), "tok", axis=0, tiled=True
    )
    attended = attention(queries, key_values)
    attended_full = lax.all_gather(attended, "wid", axis=1, tiled=True)
    projected = jnp.dot(attended_full, w_cols, preferred_element_type=jnp.float32)
    return (
        residual_in.astype(jnp.float32) + modulation[2].astype(jnp.float32)[None, :] * projected
    ).astype(jnp.bfloat16)


def solution(mesh):
    return jax.shard_map(
        body,
        mesh=mesh,
        in_specs=(
            P("tok", "wid"),
            P("tok"),
            P(),
            P("wid"),
            P(None, None, "wid"),
            P("tok", None, "wid"),
            P("wid", None),
        ),
        out_specs=P("tok", "wid"),
        check_vma=False,
    )
```

```python
import math

import jax
import jax.numpy as jnp
from jax import lax
from jax.experimental import pallas as pl
from jax.experimental.pallas import tpu as pltpu
from jax.sharding import PartitionSpec as P

D = 3072
DH = 128
TEMB = 256


def finish_rows(values, row_mean, row_var, shift_row, scale_row):
    normal = (values - row_mean) * lax.rsqrt(row_var + 1e-06)
    return (normal * (1.0 + scale_row.astype(jnp.float32)) + shift_row.astype(jnp.float32)).astype(
        jnp.bfloat16
    )


def attention_kernel(q_ref, kv0_ref, kv1_ref, o_ref):
    queries = q_ref[...]
    score_parts = [
        lax.dot_general(
            queries, kv_ref[:, :DH], (((1,), (1,)), ((), ())), preferred_element_type=jnp.float32
        )
        * (DH ** (-0.5))
        for kv_ref in (kv0_ref, kv1_ref)
    ]
    row_max = jnp.maximum(
        jnp.max(score_parts[0], axis=1, keepdims=True), jnp.max(score_parts[1], axis=1, keepdims=True)
    )
    shifted = [jnp.exp(part - row_max) for part in score_parts]
    row_sum = jnp.sum(shifted[0], axis=1, keepdims=True) + jnp.sum(shifted[1], axis=1, keepdims=True)
    numer = jnp.dot(
        shifted[0].astype(jnp.bfloat16), kv0_ref[:, DH:], preferred_element_type=jnp.float32
    ) + jnp.dot(shifted[1].astype(jnp.bfloat16), kv1_ref[:, DH:], preferred_element_type=jnp.float32)
    o_ref[...] = (numer / row_sum).astype(o_ref.dtype)


def attention(queries, kv0, kv1, block=256):
    rows = queries.shape[0]
    count = kv0.shape[0]
    return pl.pallas_call(
        attention_kernel,
        grid=(rows // block,),
        in_specs=[
            pl.BlockSpec((block, DH), lambda i: (i, 0)),
            pl.BlockSpec((count, 2 * DH), lambda i: (0, 0)),
            pl.BlockSpec((count, 2 * DH), lambda i: (0, 0)),
        ],
        out_specs=pl.BlockSpec((block, DH), lambda i: (i, 0)),
        out_shape=jax.ShapeDtypeStruct((rows, DH), jnp.bfloat16),
        compiler_params=pltpu.CompilerParams(vmem_limit_bytes=56 * 1024 * 1024),
        cost_estimate=pl.CostEstimate(
            flops=8 * rows * count * DH,
            transcendentals=2 * rows * count,
            bytes_accessed=4 * rows * DH + 8 * count * DH,
        ),
    )(queries, kv0, kv1)


def body(tokens, defect_mask, timestep, mask_embed, mod_weight, w_qkv, w_out):
    tok_rows = tokens.shape[0]
    half = tok_rows // 2
    residual_in = (
        tokens.astype(jnp.float32)
        + defect_mask.astype(jnp.float32)[:, None] * mask_embed.astype(jnp.float32)[None, :]
    ).astype(jnp.bfloat16)
    w_cols = lax.all_to_all(w_out, "wid", split_axis=1, concat_axis=0, tiled=True)
    tok_count = lax.axis_size("tok")
    w_copies = jnp.broadcast_to(w_qkv[None], (tok_count,) + w_qkv.shape)
    w_full = lax.all_to_all(w_copies, "tok", split_axis=0, concat_axis=0, tiled=True)
    w_full = w_full.reshape((tok_count * w_qkv.shape[0],) + w_qkv.shape[1:])
    half_width = TEMB // 2
    frequency = jnp.exp(-math.log(10000.0) * jnp.arange(half_width, dtype=jnp.float32) / half_width)
    angles = timestep.astype(jnp.float32)[0] * frequency
    embedding = jnp.concatenate([jnp.cos(angles), jnp.sin(angles)])
    modulation = jnp.einsum(
        "e,ecf->cf",
        jax.nn.silu(embedding),
        mod_weight.astype(jnp.float32),
        precision=lax.Precision.HIGHEST,
    ).astype(jnp.bfloat16)
    extra = jnp.zeros((16, residual_in.shape[1]), jnp.bfloat16).at[:2].set(modulation[:2])
    gathered = [
        lax.all_gather(
            jnp.concatenate([residual_in[chunk * half : (chunk + 1) * half], extra], axis=0),
            "wid",
            axis=1,
            tiled=True,
        )
        for chunk in range(2)
    ]
    queries = []
    key_values = []
    for packed in gathered:
        shift_scale = packed[half : half + 2]
        values = packed[:half].astype(jnp.float32)
        row_mean = jnp.mean(values, axis=1, keepdims=True)
        row_var = jnp.mean(values * values, axis=1, keepdims=True) - row_mean * row_mean
        normed = finish_rows(
            values, row_mean, row_var, shift_scale[0][None, :], shift_scale[1][None, :]
        )
        qkv = jnp.einsum(
            "td,dcf->tcf",
            normed,
            w_full,
            preferred_element_type=jnp.float32,
        ).astype(jnp.bfloat16)
        queries.append(qkv[:, 0])
        key_values.append(
            lax.all_gather(qkv[:, 1:3].reshape(half, 2 * DH), "tok", axis=0, tiled=True)
        )
    key_values[1], w_cols = lax.optimization_barrier((key_values[1], w_cols))
    gate = modulation[2].astype(jnp.float32)[None, :]
    outputs = []
    for chunk, query_rows in enumerate(queries):
        attended = attention(query_rows, key_values[0], key_values[1])
        attended_full = lax.all_gather(attended, "wid", axis=1, tiled=True)
        projected = jnp.dot(attended_full, w_cols, preferred_element_type=jnp.float32)
        rows = residual_in[chunk * half : (chunk + 1) * half]
        outputs.append((rows.astype(jnp.float32) + gate * projected).astype(jnp.bfloat16))
    return jnp.concatenate(outputs, axis=0)


def solution(mesh):
    return jax.shard_map(
        body,
        mesh=mesh,
        in_specs=(
            P("tok", "wid"),
            P("tok"),
            P(),
            P("wid"),
            P(None, None, "wid"),
            P("tok", None, "wid"),
            P("wid", None),
        ),
        out_specs=P("tok", "wid"),
        check_vma=False,
    )
```

```python
import math

import jax
import jax.numpy as jnp
from jax import lax
from jax.experimental import pallas as pl
from jax.experimental.pallas import tpu as pltpu
from jax.sharding import PartitionSpec as P

D = 3072
DH = 128
TEMB = 256


def finish_rows(values, row_mean, row_var, shift_row, scale_row):
    normal = (values - row_mean) * lax.rsqrt(row_var + 1e-06)
    return (normal * (1.0 + scale_row.astype(jnp.float32)) + shift_row.astype(jnp.float32)).astype(
        jnp.bfloat16
    )


def attention_kernel(q_ref, kv_ref, o_ref):
    keys = kv_ref[:, :DH]
    values = kv_ref[:, DH:]
    scores = lax.dot_general(
        q_ref[...], keys, (((1,), (1,)), ((), ())), preferred_element_type=jnp.float32
    ) * (DH ** (-0.5))
    shifted = jnp.exp(scores - jnp.max(scores, axis=1, keepdims=True))
    row_sum = jnp.sum(shifted, axis=1, keepdims=True)
    numer = jnp.dot(shifted.astype(jnp.bfloat16), values, preferred_element_type=jnp.float32)
    o_ref[...] = (numer / row_sum).astype(o_ref.dtype)


def attention(queries, key_values, block=256):
    rows = queries.shape[0]
    count = key_values.shape[0]
    return pl.pallas_call(
        attention_kernel,
        grid=(rows // block,),
        in_specs=[
            pl.BlockSpec((block, DH), lambda i: (i, 0)),
            pl.BlockSpec((count, 2 * DH), lambda i: (0, 0)),
        ],
        out_specs=pl.BlockSpec((block, DH), lambda i: (i, 0)),
        out_shape=jax.ShapeDtypeStruct((rows, DH), jnp.bfloat16),
        compiler_params=pltpu.CompilerParams(vmem_limit_bytes=56 * 1024 * 1024),
        cost_estimate=pl.CostEstimate(
            flops=4 * rows * count * DH,
            transcendentals=rows * count,
            bytes_accessed=4 * rows * DH + 4 * count * DH,
        ),
    )(queries, key_values)


def body(tokens, defect_mask, timestep, mask_embed, mod_weight, w_qkv, w_out):
    tok_rows = tokens.shape[0]
    residual_in = (
        tokens.astype(jnp.float32)
        + defect_mask.astype(jnp.float32)[:, None] * mask_embed.astype(jnp.float32)[None, :]
    ).astype(jnp.bfloat16)
    tok_count = lax.axis_size("tok")
    w_copies = jnp.broadcast_to(w_qkv[None], (tok_count,) + w_qkv.shape)
    w_full = lax.all_to_all(w_copies, "tok", split_axis=0, concat_axis=0, tiled=True)
    w_full = w_full.reshape((tok_count * w_qkv.shape[0],) + w_qkv.shape[1:])
    half_width = TEMB // 2
    frequency = jnp.exp(-math.log(10000.0) * jnp.arange(half_width, dtype=jnp.float32) / half_width)
    angles = timestep.astype(jnp.float32)[0] * frequency
    embedding = jnp.concatenate([jnp.cos(angles), jnp.sin(angles)])
    modulation = jnp.einsum(
        "e,ecf->cf",
        jax.nn.silu(embedding),
        mod_weight.astype(jnp.float32),
        precision=lax.Precision.HIGHEST,
    ).astype(jnp.bfloat16)
    extra = jnp.zeros((16, residual_in.shape[1]), jnp.bfloat16).at[:2].set(modulation[:2])
    packed = lax.all_gather(
        jnp.concatenate([residual_in, extra], axis=0), "wid", axis=1, tiled=True
    )
    residual_full = packed[:tok_rows]
    shift_scale = packed[tok_rows : tok_rows + 2]
    values = residual_full.astype(jnp.float32)
    row_mean = jnp.mean(values, axis=1, keepdims=True)
    row_var = jnp.mean(values * values, axis=1, keepdims=True) - row_mean * row_mean
    normed = finish_rows(values, row_mean, row_var, shift_scale[0][None, :], shift_scale[1][None, :])
    qkv = jnp.einsum(
        "td,dcf->tcf",
        normed,
        w_full,
        preferred_element_type=jnp.float32,
    ).astype(jnp.bfloat16)
    w_late, qkv = lax.optimization_barrier((w_out, qkv))
    w_cols = lax.all_to_all(w_late, "wid", split_axis=1, concat_axis=0, tiled=True)
    queries = qkv[:, 0]
    key_values = lax.all_gather(
        qkv[:, 1:3].reshape(tok_rows, 2 * DH), "tok", axis=0, tiled=True
    )
    w_cols, key_values = lax.optimization_barrier((w_cols, key_values))
    attended = attention(queries, key_values)
    attended_full = lax.all_gather(attended, "wid", axis=1, tiled=True)
    projected = jnp.dot(attended_full, w_cols, preferred_element_type=jnp.float32)
    return (
        residual_in.astype(jnp.float32) + modulation[2].astype(jnp.float32)[None, :] * projected
    ).astype(jnp.bfloat16)


def solution(mesh):
    return jax.shard_map(
        body,
        mesh=mesh,
        in_specs=(
            P("tok", "wid"),
            P("tok"),
            P(),
            P("wid"),
            P(None, None, "wid"),
            P("tok", None, "wid"),
            P("wid", None),
        ),
        out_specs=P("tok", "wid"),
        check_vma=False,
    )
```

```python
import math

import jax
import jax.numpy as jnp
from jax import lax
from jax.experimental import pallas as pl
from jax.experimental.pallas import tpu as pltpu
from jax.sharding import PartitionSpec as P

D = 3072
DH = 128
TEMB = 256


def finish_rows(values, row_mean, row_var, shift_row, scale_row):
    normal = (values - row_mean) * lax.rsqrt(row_var + 1e-06)
    return (normal * (1.0 + scale_row.astype(jnp.float32)) + shift_row.astype(jnp.float32)).astype(
        jnp.bfloat16
    )


def project_kernel(x_ref, mod_ref, w_ref, q_ref, kv_ref):
    values = x_ref[...].astype(jnp.float32)
    width = values.shape[1]
    row_mean = jnp.sum(values, axis=1, keepdims=True) / width
    row_var = jnp.sum(values * values, axis=1, keepdims=True) / width - row_mean * row_mean
    shift_row = mod_ref[0:1, :].astype(jnp.float32)
    scale_row = mod_ref[1:2, :].astype(jnp.float32)
    normal = (values - row_mean) * lax.rsqrt(row_var + 1e-06)
    normed = (normal * (1.0 + scale_row) + shift_row).astype(jnp.bfloat16)
    qkv = jnp.dot(normed, w_ref[...], preferred_element_type=jnp.float32).astype(jnp.bfloat16)
    q_ref[...] = qkv[:, :DH]
    kv_ref[...] = qkv[:, DH:]


def project(packed, rows, weights, block=256):
    width = packed.shape[1]
    extra_block = rows // 16
    return pl.pallas_call(
        project_kernel,
        grid=(rows // block,),
        in_specs=[
            pl.BlockSpec((block, width), lambda i: (i, 0)),
            pl.BlockSpec((16, width), lambda i: (extra_block, 0)),
            pl.BlockSpec(weights.shape, lambda i: (0, 0)),
        ],
        out_specs=[
            pl.BlockSpec((block, DH), lambda i: (i, 0)),
            pl.BlockSpec((block, 2 * DH), lambda i: (i, 0)),
        ],
        out_shape=[
            jax.ShapeDtypeStruct((rows, DH), jnp.bfloat16),
            jax.ShapeDtypeStruct((rows, 2 * DH), jnp.bfloat16),
        ],
        compiler_params=pltpu.CompilerParams(vmem_limit_bytes=48 * 1024 * 1024),
        cost_estimate=pl.CostEstimate(
            flops=2 * rows * width * weights.shape[1] + 10 * rows * width,
            transcendentals=rows,
            bytes_accessed=2 * rows * width + 2 * weights.size + 2 * rows * 3 * DH,
        ),
    )(packed, packed, weights)


def attention_kernel(q_ref, kv_ref, o_ref):
    keys = kv_ref[:, :DH]
    values = kv_ref[:, DH:]
    scores = lax.dot_general(
        q_ref[...], keys, (((1,), (1,)), ((), ())), preferred_element_type=jnp.float32
    ) * (DH ** (-0.5))
    shifted = jnp.exp(scores - jnp.max(scores, axis=1, keepdims=True))
    row_sum = jnp.sum(shifted, axis=1, keepdims=True)
    numer = jnp.dot(shifted.astype(jnp.bfloat16), values, preferred_element_type=jnp.float32)
    o_ref[...] = (numer / row_sum).astype(o_ref.dtype)


def attention(queries, key_values, block=256):
    rows = queries.shape[0]
    count = key_values.shape[0]
    return pl.pallas_call(
        attention_kernel,
        grid=(rows // block,),
        in_specs=[
            pl.BlockSpec((block, DH), lambda i: (i, 0)),
            pl.BlockSpec((count, 2 * DH), lambda i: (0, 0)),
        ],
        out_specs=pl.BlockSpec((block, DH), lambda i: (i, 0)),
        out_shape=jax.ShapeDtypeStruct((rows, DH), jnp.bfloat16),
        compiler_params=pltpu.CompilerParams(vmem_limit_bytes=56 * 1024 * 1024),
        cost_estimate=pl.CostEstimate(
            flops=4 * rows * count * DH,
            transcendentals=rows * count,
            bytes_accessed=4 * rows * DH + 4 * count * DH,
        ),
    )(queries, key_values)


def body(tokens, defect_mask, timestep, mask_embed, mod_weight, w_qkv, w_out):
    tok_rows = tokens.shape[0]
    residual_in = (
        tokens.astype(jnp.float32)
        + defect_mask.astype(jnp.float32)[:, None] * mask_embed.astype(jnp.float32)[None, :]
    ).astype(jnp.bfloat16)
    tok_count = lax.axis_size("tok")
    w_copies = jnp.broadcast_to(w_qkv[None], (tok_count,) + w_qkv.shape)
    w_full = lax.all_to_all(w_copies, "tok", split_axis=0, concat_axis=0, tiled=True)
    w_full = w_full.reshape((tok_count * w_qkv.shape[0],) + w_qkv.shape[1:])
    half_width = TEMB // 2
    frequency = jnp.exp(-math.log(10000.0) * jnp.arange(half_width, dtype=jnp.float32) / half_width)
    angles = timestep.astype(jnp.float32)[0] * frequency
    embedding = jnp.concatenate([jnp.cos(angles), jnp.sin(angles)])
    modulation = jnp.einsum(
        "e,ecf->cf",
        jax.nn.silu(embedding),
        mod_weight.astype(jnp.float32),
        precision=lax.Precision.HIGHEST,
    ).astype(jnp.bfloat16)
    extra = jnp.zeros((16, residual_in.shape[1]), jnp.bfloat16).at[:2].set(modulation[:2])
    packed = lax.all_gather(
        jnp.concatenate([residual_in, extra], axis=0), "wid", axis=1, tiled=True
    )
    queries, key_rows = project(packed, tok_rows, w_full.reshape(w_full.shape[0], 3 * DH))
    qkv = (queries, key_rows)
    w_late, qkv = lax.optimization_barrier((w_out, qkv))
    w_cols = lax.all_to_all(w_late, "wid", split_axis=1, concat_axis=0, tiled=True)
    queries, key_rows = qkv
    key_values = lax.all_gather(key_rows, "tok", axis=0, tiled=True)
    w_cols, key_values = lax.optimization_barrier((w_cols, key_values))
    attended = attention(queries, key_values)
    attended_full = lax.all_gather(attended, "wid", axis=1, tiled=True)
    projected = jnp.dot(attended_full, w_cols, preferred_element_type=jnp.float32)
    return (
        residual_in.astype(jnp.float32) + modulation[2].astype(jnp.float32)[None, :] * projected
    ).astype(jnp.bfloat16)


def solution(mesh):
    return jax.shard_map(
        body,
        mesh=mesh,
        in_specs=(
            P("tok", "wid"),
            P("tok"),
            P(),
            P("wid"),
            P(None, None, "wid"),
            P("tok", None, "wid"),
            P("wid", None),
        ),
        out_specs=P("tok", "wid"),
        check_vma=False,
    )
```

```python
import math

import jax
import jax.numpy as jnp
from jax import lax
from jax.experimental import pallas as pl
from jax.experimental.pallas import tpu as pltpu
from jax.sharding import PartitionSpec as P

D = 3072
DH = 128
TEMB = 256


def finish_rows(values, row_mean, row_var, shift_row, scale_row):
    normal = (values - row_mean) * lax.rsqrt(row_var + 1e-06)
    return (normal * (1.0 + scale_row.astype(jnp.float32)) + shift_row.astype(jnp.float32)).astype(
        jnp.bfloat16
    )


def attention_kernel(q_ref, kv_ref, o_ref):
    keys = kv_ref[:, :DH]
    values = kv_ref[:, DH:]
    scores = lax.dot_general(
        q_ref[...], keys, (((1,), (1,)), ((), ())), preferred_element_type=jnp.float32
    ) * (DH ** (-0.5))
    shifted = jnp.exp(scores - jnp.max(scores, axis=1, keepdims=True))
    row_sum = jnp.sum(shifted, axis=1, keepdims=True)
    numer = jnp.dot(shifted.astype(jnp.bfloat16), values, preferred_element_type=jnp.float32)
    o_ref[...] = (numer / row_sum).astype(o_ref.dtype)


def attention(queries, key_values, block=256):
    rows = queries.shape[0]
    count = key_values.shape[0]
    return pl.pallas_call(
        attention_kernel,
        grid=(rows // block,),
        in_specs=[
            pl.BlockSpec((block, DH), lambda i: (i, 0)),
            pl.BlockSpec((count, 2 * DH), lambda i: (0, 0)),
        ],
        out_specs=pl.BlockSpec((block, DH), lambda i: (i, 0)),
        out_shape=jax.ShapeDtypeStruct((rows, DH), jnp.bfloat16),
        compiler_params=pltpu.CompilerParams(vmem_limit_bytes=56 * 1024 * 1024),
        cost_estimate=pl.CostEstimate(
            flops=4 * rows * count * DH,
            transcendentals=rows * count,
            bytes_accessed=4 * rows * DH + 4 * count * DH,
        ),
    )(queries, key_values)


def body(tokens, defect_mask, timestep, mask_embed, mod_weight, w_qkv, w_out):
    tok_rows = tokens.shape[0]
    residual_in = (
        tokens.astype(jnp.float32)
        + defect_mask.astype(jnp.float32)[:, None] * mask_embed.astype(jnp.float32)[None, :]
    ).astype(jnp.bfloat16)
    tok_count = lax.axis_size("tok")
    w_copies = jnp.broadcast_to(w_qkv[None], (tok_count,) + w_qkv.shape)
    w_full = lax.all_to_all(w_copies, "tok", split_axis=0, concat_axis=0, tiled=True)
    w_full = w_full.reshape((tok_count * w_qkv.shape[0],) + w_qkv.shape[1:])
    half_width = TEMB // 2
    frequency = jnp.exp(-math.log(10000.0) * jnp.arange(half_width, dtype=jnp.float32) / half_width)
    angles = timestep.astype(jnp.float32)[0] * frequency
    embedding = jnp.concatenate([jnp.cos(angles), jnp.sin(angles)])
    modulation = jnp.einsum(
        "e,ecf->cf",
        jax.nn.silu(embedding),
        mod_weight.astype(jnp.float32),
        precision=lax.Precision.HIGHEST,
    ).astype(jnp.bfloat16)
    extra = jnp.zeros((16, residual_in.shape[1]), jnp.bfloat16).at[:2].set(modulation[:2])
    packed = lax.all_gather(
        jnp.concatenate([residual_in, extra], axis=0), "wid", axis=1, tiled=True
    )
    residual_full = packed[:tok_rows]
    shift_scale = packed[tok_rows : tok_rows + 2]
    values = residual_full.astype(jnp.float32)
    row_mean = jnp.mean(values, axis=1, keepdims=True)
    row_var = jnp.mean(values * values, axis=1, keepdims=True) - row_mean * row_mean
    normed = finish_rows(values, row_mean, row_var, shift_scale[0][None, :], shift_scale[1][None, :])
    qkv = jnp.einsum(
        "td,dcf->tcf",
        normed,
        w_full,
        preferred_element_type=jnp.float32,
    ).astype(jnp.bfloat16)
    w_late, qkv = lax.optimization_barrier((w_out, qkv))
    w_cols = lax.all_to_all(w_late, "wid", split_axis=1, concat_axis=0, tiled=True)
    queries = qkv[:, 0]
    key_values = lax.all_gather(
        qkv[:, 1:3].reshape(tok_rows, 2 * DH), "tok", axis=0, tiled=True
    )
    w_cols, key_values = lax.optimization_barrier((w_cols, key_values))
    attended = attention(queries, key_values)
    heads = lax.all_gather(attended, "wid", axis=0, tiled=False)
    projected = jnp.einsum(
        "htd,hdc->tc",
        heads,
        w_cols.reshape(heads.shape[0], DH, w_cols.shape[1]),
        preferred_element_type=jnp.float32,
    )
    return (
        residual_in.astype(jnp.float32) + modulation[2].astype(jnp.float32)[None, :] * projected
    ).astype(jnp.bfloat16)


def solution(mesh):
    return jax.shard_map(
        body,
        mesh=mesh,
        in_specs=(
            P("tok", "wid"),
            P("tok"),
            P(),
            P("wid"),
            P(None, None, "wid"),
            P("tok", None, "wid"),
            P("wid", None),
        ),
        out_specs=P("tok", "wid"),
        check_vma=False,
    )
```

```python
import math

import jax
import jax.numpy as jnp
from jax import lax
from jax.experimental import pallas as pl
from jax.experimental.pallas import tpu as pltpu
from jax.sharding import PartitionSpec as P

D = 3072
DH = 128
TEMB = 256


def finish_rows(values, row_mean, row_var, shift_row, scale_row):
    normal = (values - row_mean) * lax.rsqrt(row_var + 1e-06)
    return (normal * (1.0 + scale_row.astype(jnp.float32)) + shift_row.astype(jnp.float32)).astype(
        jnp.bfloat16
    )


def attention_kernel(q_ref, kv_ref, o_ref):
    keys = kv_ref[:, :DH]
    values = kv_ref[:, DH:]
    scores = lax.dot_general(
        q_ref[...], keys, (((1,), (1,)), ((), ())), preferred_element_type=jnp.float32
    ) * (DH ** (-0.5))
    shifted = jnp.exp(scores - jnp.max(scores, axis=1, keepdims=True))
    row_sum = jnp.sum(shifted, axis=1, keepdims=True)
    numer = jnp.dot(shifted.astype(jnp.bfloat16), values, preferred_element_type=jnp.float32)
    o_ref[...] = (numer / row_sum).astype(o_ref.dtype)


def attention(queries, key_values, block=256):
    rows = queries.shape[0]
    count = key_values.shape[0]
    return pl.pallas_call(
        attention_kernel,
        grid=(rows // block,),
        in_specs=[
            pl.BlockSpec((block, DH), lambda i: (i, 0)),
            pl.BlockSpec((count, 2 * DH), lambda i: (0, 0)),
        ],
        out_specs=pl.BlockSpec((block, DH), lambda i: (i, 0)),
        out_shape=jax.ShapeDtypeStruct((rows, DH), jnp.bfloat16),
        compiler_params=pltpu.CompilerParams(vmem_limit_bytes=56 * 1024 * 1024),
        cost_estimate=pl.CostEstimate(
            flops=4 * rows * count * DH,
            transcendentals=rows * count,
            bytes_accessed=4 * rows * DH + 4 * count * DH,
        ),
    )(queries, key_values)


def body(tokens, defect_mask, timestep, mask_embed, mod_weight, w_qkv, w_out):
    tok_rows = tokens.shape[0]
    residual_in = (
        tokens.astype(jnp.float32)
        + defect_mask.astype(jnp.float32)[:, None] * mask_embed.astype(jnp.float32)[None, :]
    ).astype(jnp.bfloat16)
    tok_count = lax.axis_size("tok")
    w_copies = jnp.broadcast_to(w_qkv[None], (tok_count,) + w_qkv.shape)
    w_full = lax.all_to_all(w_copies, "tok", split_axis=0, concat_axis=0, tiled=True)
    w_full = w_full.reshape((tok_count * w_qkv.shape[0],) + w_qkv.shape[1:])
    half_width = TEMB // 2
    frequency = jnp.exp(-math.log(10000.0) * jnp.arange(half_width, dtype=jnp.float32) / half_width)
    angles = timestep.astype(jnp.float32)[0] * frequency
    embedding = jnp.concatenate([jnp.cos(angles), jnp.sin(angles)])
    modulation = jnp.einsum(
        "e,ecf->cf",
        jax.nn.silu(embedding),
        mod_weight.astype(jnp.float32),
        precision=lax.Precision.HIGHEST,
    ).astype(jnp.bfloat16)
    extra = jnp.zeros((16, residual_in.shape[1]), jnp.bfloat16).at[:2].set(modulation[:2])
    stacked = lax.all_gather(
        jnp.concatenate([residual_in, extra], axis=0), "wid", axis=0, tiled=False
    )
    values = stacked[:, :tok_rows, :].astype(jnp.float32)
    shift_rows = stacked[:, tok_rows : tok_rows + 1, :]
    scale_rows = stacked[:, tok_rows + 1 : tok_rows + 2, :]
    row_mean = jnp.sum(values, axis=(0, 2), keepdims=True) / D
    row_var = jnp.sum(values * values, axis=(0, 2), keepdims=True) / D - row_mean * row_mean
    normed = finish_rows(values, row_mean, row_var, shift_rows, scale_rows)
    qkv = jnp.einsum(
        "jtc,jcf->tf",
        normed,
        w_full.reshape(stacked.shape[0], stacked.shape[2], 3 * DH),
        preferred_element_type=jnp.float32,
    ).astype(jnp.bfloat16)
    w_late, qkv = lax.optimization_barrier((w_out, qkv))
    w_cols = lax.all_to_all(w_late, "wid", split_axis=1, concat_axis=0, tiled=True)
    queries = qkv[:, :DH]
    key_values = lax.all_gather(qkv[:, DH:], "tok", axis=0, tiled=True)
    w_cols, key_values = lax.optimization_barrier((w_cols, key_values))
    attended = attention(queries, key_values)
    heads = lax.all_gather(attended, "wid", axis=0, tiled=False)
    projected = jnp.einsum(
        "htd,hdc->tc",
        heads,
        w_cols.reshape(heads.shape[0], DH, w_cols.shape[1]),
        preferred_element_type=jnp.float32,
    )
    return (
        residual_in.astype(jnp.float32) + modulation[2].astype(jnp.float32)[None, :] * projected
    ).astype(jnp.bfloat16)


def solution(mesh):
    return jax.shard_map(
        body,
        mesh=mesh,
        in_specs=(
            P("tok", "wid"),
            P("tok"),
            P(),
            P("wid"),
            P(None, None, "wid"),
            P("tok", None, "wid"),
            P("wid", None),
        ),
        out_specs=P("tok", "wid"),
        check_vma=False,
    )
```

```python
import math

import jax
import jax.numpy as jnp
from jax import lax
from jax.experimental import pallas as pl
from jax.experimental.pallas import tpu as pltpu
from jax.sharding import PartitionSpec as P

D = 3072
DH = 128
TEMB = 256


def finish_rows(values, row_mean, row_var, shift_row, scale_row):
    normal = (values - row_mean) * lax.rsqrt(row_var + 1e-06)
    return (normal * (1.0 + scale_row.astype(jnp.float32)) + shift_row.astype(jnp.float32)).astype(
        jnp.bfloat16
    )


def attention_kernel(q_ref, kv_ref, o_ref):
    keys = kv_ref[:, :DH]
    values = kv_ref[:, DH:]
    scores = lax.dot_general(
        q_ref[...], keys, (((1,), (1,)), ((), ())), preferred_element_type=jnp.float32
    ) * (DH ** (-0.5))
    shifted = jnp.exp(scores - jnp.max(scores, axis=1, keepdims=True))
    row_sum = jnp.sum(shifted, axis=1, keepdims=True)
    numer = jnp.dot(shifted.astype(jnp.bfloat16), values, preferred_element_type=jnp.float32)
    o_ref[...] = (numer / row_sum).astype(o_ref.dtype)


def attention(queries, key_values, block=256):
    rows = queries.shape[0]
    count = key_values.shape[0]
    return pl.pallas_call(
        attention_kernel,
        grid=(rows // block,),
        in_specs=[
            pl.BlockSpec((block, DH), lambda i: (i, 0)),
            pl.BlockSpec((count, 2 * DH), lambda i: (0, 0)),
        ],
        out_specs=pl.BlockSpec((block, DH), lambda i: (i, 0)),
        out_shape=jax.ShapeDtypeStruct((rows, DH), jnp.bfloat16),
        compiler_params=pltpu.CompilerParams(vmem_limit_bytes=56 * 1024 * 1024),
        cost_estimate=pl.CostEstimate(
            flops=4 * rows * count * DH,
            transcendentals=rows * count,
            bytes_accessed=4 * rows * DH + 4 * count * DH,
        ),
    )(queries, key_values)


def body(tokens, defect_mask, timestep, mask_embed, mod_weight, w_qkv, w_out):
    tok_rows = tokens.shape[0]
    residual_in = (
        tokens.astype(jnp.float32)
        + defect_mask.astype(jnp.float32)[:, None] * mask_embed.astype(jnp.float32)[None, :]
    ).astype(jnp.bfloat16)
    tok_count = lax.axis_size("tok")
    w_copies = jnp.broadcast_to(w_qkv[None], (tok_count,) + w_qkv.shape)
    w_full = lax.all_to_all(w_copies, "tok", split_axis=0, concat_axis=0, tiled=True)
    w_full = w_full.reshape((tok_count * w_qkv.shape[0],) + w_qkv.shape[1:])
    half_width = TEMB // 2
    frequency = jnp.exp(-math.log(10000.0) * jnp.arange(half_width, dtype=jnp.float32) / half_width)
    angles = timestep.astype(jnp.float32)[0] * frequency
    embedding = jnp.concatenate([jnp.cos(angles), jnp.sin(angles)])
    modulation = jnp.einsum(
        "e,ecf->cf",
        jax.nn.silu(embedding),
        mod_weight.astype(jnp.float32),
        precision=lax.Precision.HIGHEST,
    ).astype(jnp.bfloat16)
    residual_full = lax.all_gather(residual_in, "wid", axis=1, tiled=True)
    wid_count = lax.axis_size("wid")
    mod_copies = jnp.broadcast_to(modulation[None, :2], (wid_count, 2, modulation.shape[1]))
    mod_parts = lax.all_to_all(mod_copies, "wid", split_axis=0, concat_axis=0, tiled=True)
    shift_scale = jnp.transpose(mod_parts, (1, 0, 2)).reshape(2, wid_count * modulation.shape[1])
    values = residual_full.astype(jnp.float32)
    row_mean = jnp.mean(values, axis=1, keepdims=True)
    row_var = jnp.mean(values * values, axis=1, keepdims=True) - row_mean * row_mean
    normed = finish_rows(values, row_mean, row_var, shift_scale[0][None, :], shift_scale[1][None, :])
    qkv = jnp.einsum(
        "td,dcf->tcf",
        normed,
        w_full,
        preferred_element_type=jnp.float32,
    ).astype(jnp.bfloat16)
    w_late, qkv = lax.optimization_barrier((w_out, qkv))
    w_cols = lax.all_to_all(w_late, "wid", split_axis=1, concat_axis=0, tiled=True)
    queries = qkv[:, 0]
    key_values = lax.all_gather(
        qkv[:, 1:3].reshape(tok_rows, 2 * DH), "tok", axis=0, tiled=True
    )
    w_cols, key_values = lax.optimization_barrier((w_cols, key_values))
    attended = attention(queries, key_values)
    heads = lax.all_gather(attended, "wid", axis=0, tiled=False)
    projected = jnp.einsum(
        "htd,hdc->tc",
        heads,
        w_cols.reshape(heads.shape[0], DH, w_cols.shape[1]),
        preferred_element_type=jnp.float32,
    )
    return (
        residual_in.astype(jnp.float32) + modulation[2].astype(jnp.float32)[None, :] * projected
    ).astype(jnp.bfloat16)


def solution(mesh):
    return jax.shard_map(
        body,
        mesh=mesh,
        in_specs=(
            P("tok", "wid"),
            P("tok"),
            P(),
            P("wid"),
            P(None, None, "wid"),
            P("tok", None, "wid"),
            P("wid", None),
        ),
        out_specs=P("tok", "wid"),
        check_vma=False,
    )
```

```python
import math

import jax
import jax.numpy as jnp
from jax import lax
from jax.experimental import pallas as pl
from jax.experimental.pallas import tpu as pltpu
from jax.sharding import PartitionSpec as P

D = 3072
DH = 128
TEMB = 256


def finish_rows(values, row_mean, row_var, shift_row, scale_row):
    normal = (values - row_mean) * lax.rsqrt(row_var + 1e-06)
    return (normal * (1.0 + scale_row.astype(jnp.float32)) + shift_row.astype(jnp.float32)).astype(
        jnp.bfloat16
    )


def project_kernel(x_ref, mod_ref, w_ref, o_ref):
    values = x_ref[...].astype(jnp.float32)
    width = values.shape[0]
    row_mean = jnp.sum(values, axis=0, keepdims=True) / width
    row_var = jnp.sum(values * values, axis=0, keepdims=True) / width - row_mean * row_mean
    normal = (values - row_mean) * lax.rsqrt(row_var + 1e-06)
    shift_col = mod_ref[:, 0:1].astype(jnp.float32)
    scale_col = mod_ref[:, 1:2].astype(jnp.float32)
    normed = (normal * (1.0 + scale_col) + shift_col).astype(jnp.bfloat16)
    o_ref[...] = jnp.dot(w_ref[...], normed, preferred_element_type=jnp.float32).astype(o_ref.dtype)


def project(rows_t, mod_cols, weights_t, block=256):
    width, rows = rows_t.shape
    outs = weights_t.shape[0]
    return pl.pallas_call(
        project_kernel,
        grid=(rows // block,),
        in_specs=[
            pl.BlockSpec((width, block), lambda i: (0, i)),
            pl.BlockSpec(mod_cols.shape, lambda i: (0, 0)),
            pl.BlockSpec(weights_t.shape, lambda i: (0, 0)),
        ],
        out_specs=pl.BlockSpec((outs, block), lambda i: (0, i)),
        out_shape=jax.ShapeDtypeStruct((outs, rows), jnp.bfloat16),
        compiler_params=pltpu.CompilerParams(vmem_limit_bytes=48 * 1024 * 1024),
        cost_estimate=pl.CostEstimate(
            flops=2 * rows * width * outs + 10 * rows * width,
            transcendentals=rows,
            bytes_accessed=2 * rows * width + 2 * width * outs + 2 * rows * outs,
        ),
    )(rows_t, mod_cols, weights_t)


def attention_kernel(q_ref, kv_ref, o_ref):
    keys = kv_ref[:, :DH]
    values = kv_ref[:, DH:]
    scores = lax.dot_general(
        q_ref[...], keys, (((1,), (1,)), ((), ())), preferred_element_type=jnp.float32
    ) * (DH ** (-0.5))
    shifted = jnp.exp(scores - jnp.max(scores, axis=1, keepdims=True))
    row_sum = jnp.sum(shifted, axis=1, keepdims=True)
    numer = jnp.dot(shifted.astype(jnp.bfloat16), values, preferred_element_type=jnp.float32)
    o_ref[...] = (numer / row_sum).astype(o_ref.dtype)


def attention(queries, key_values, block=256):
    rows = queries.shape[0]
    count = key_values.shape[0]
    return pl.pallas_call(
        attention_kernel,
        grid=(rows // block,),
        in_specs=[
            pl.BlockSpec((block, DH), lambda i: (i, 0)),
            pl.BlockSpec((count, 2 * DH), lambda i: (0, 0)),
        ],
        out_specs=pl.BlockSpec((block, DH), lambda i: (i, 0)),
        out_shape=jax.ShapeDtypeStruct((rows, DH), jnp.bfloat16),
        compiler_params=pltpu.CompilerParams(vmem_limit_bytes=56 * 1024 * 1024),
        cost_estimate=pl.CostEstimate(
            flops=4 * rows * count * DH,
            transcendentals=rows * count,
            bytes_accessed=4 * rows * DH + 4 * count * DH,
        ),
    )(queries, key_values)


def body(tokens, defect_mask, timestep, mask_embed, mod_weight, w_qkv, w_out):
    tok_rows = tokens.shape[0]
    residual_in = (
        tokens.astype(jnp.float32)
        + defect_mask.astype(jnp.float32)[:, None] * mask_embed.astype(jnp.float32)[None, :]
    ).astype(jnp.bfloat16)
    tok_count = lax.axis_size("tok")
    w_copies = jnp.broadcast_to(w_qkv[None], (tok_count,) + w_qkv.shape)
    w_full = lax.all_to_all(w_copies, "tok", split_axis=0, concat_axis=0, tiled=True)
    w_full = w_full.reshape((tok_count * w_qkv.shape[0],) + w_qkv.shape[1:])
    half_width = TEMB // 2
    frequency = jnp.exp(-math.log(10000.0) * jnp.arange(half_width, dtype=jnp.float32) / half_width)
    angles = timestep.astype(jnp.float32)[0] * frequency
    embedding = jnp.concatenate([jnp.cos(angles), jnp.sin(angles)])
    modulation = jnp.einsum(
        "e,ecf->cf",
        jax.nn.silu(embedding),
        mod_weight.astype(jnp.float32),
        precision=lax.Precision.HIGHEST,
    ).astype(jnp.bfloat16)
    residual_full = lax.all_gather(residual_in, "wid", axis=1, tiled=True)
    wid_count = lax.axis_size("wid")
    mod_copies = jnp.broadcast_to(modulation[None, :2], (wid_count, 2, modulation.shape[1]))
    mod_parts = lax.all_to_all(mod_copies, "wid", split_axis=0, concat_axis=0, tiled=True)
    shift_scale = jnp.transpose(mod_parts, (1, 0, 2)).reshape(2, wid_count * modulation.shape[1])
    weights_t = w_full.reshape(w_full.shape[0], 3 * DH).T
    qkv_t = project(residual_full.T, shift_scale.T, weights_t)
    qkv = (qkv_t[:DH].T, qkv_t[DH:].T)
    w_late, qkv = lax.optimization_barrier((w_out, qkv))
    w_cols = lax.all_to_all(w_late, "wid", split_axis=1, concat_axis=0, tiled=True)
    queries, key_rows = qkv
    key_values = lax.all_gather(key_rows, "tok", axis=0, tiled=True)
    w_cols, key_values = lax.optimization_barrier((w_cols, key_values))
    attended = attention(queries, key_values)
    heads = lax.all_gather(attended, "wid", axis=0, tiled=False)
    projected = jnp.einsum(
        "htd,hdc->tc",
        heads,
        w_cols.reshape(heads.shape[0], DH, w_cols.shape[1]),
        preferred_element_type=jnp.float32,
    )
    return (
        residual_in.astype(jnp.float32) + modulation[2].astype(jnp.float32)[None, :] * projected
    ).astype(jnp.bfloat16)


def solution(mesh):
    return jax.shard_map(
        body,
        mesh=mesh,
        in_specs=(
            P("tok", "wid"),
            P("tok"),
            P(),
            P("wid"),
            P(None, None, "wid"),
            P("tok", None, "wid"),
            P("wid", None),
        ),
        out_specs=P("tok", "wid"),
        check_vma=False,
    )
```

```python
import math

import jax
import jax.numpy as jnp
from jax import lax
from jax.experimental import pallas as pl
from jax.experimental.pallas import tpu as pltpu
from jax.sharding import PartitionSpec as P

D = 3072
DH = 128
TEMB = 256


def finish_rows(values, row_mean, row_var, shift_row, scale_row):
    normal = (values - row_mean) * lax.rsqrt(row_var + 1e-06)
    return (normal * (1.0 + scale_row.astype(jnp.float32)) + shift_row.astype(jnp.float32)).astype(
        jnp.bfloat16
    )


def project_kernel(x_ref, mod_ref, w_ref, q_ref, kv_ref):
    values = x_ref[...].astype(jnp.float32)
    width = values.shape[0]
    row_mean = jnp.sum(values, axis=0, keepdims=True) / width
    row_var = jnp.sum(values * values, axis=0, keepdims=True) / width - row_mean * row_mean
    normal = (values - row_mean) * lax.rsqrt(row_var + 1e-06)
    shift_col = mod_ref[:, 0:1].astype(jnp.float32)
    scale_col = mod_ref[:, 1:2].astype(jnp.float32)
    normed = (normal * (1.0 + scale_col) + shift_col).astype(jnp.bfloat16)
    qkv_t = jnp.dot(w_ref[...], normed, preferred_element_type=jnp.float32)
    qkv = jnp.transpose(qkv_t).astype(jnp.bfloat16)
    q_ref[...] = qkv[:, :DH]
    kv_ref[...] = qkv[:, DH:]


def project(rows_t, mod_cols, weights_t, block=256):
    width, rows = rows_t.shape
    outs = weights_t.shape[0]
    return pl.pallas_call(
        project_kernel,
        grid=(rows // block,),
        in_specs=[
            pl.BlockSpec((width, block), lambda i: (0, i)),
            pl.BlockSpec(mod_cols.shape, lambda i: (0, 0)),
            pl.BlockSpec(weights_t.shape, lambda i: (0, 0)),
        ],
        out_specs=[
            pl.BlockSpec((block, DH), lambda i: (i, 0)),
            pl.BlockSpec((block, outs - DH), lambda i: (i, 0)),
        ],
        out_shape=[
            jax.ShapeDtypeStruct((rows, DH), jnp.bfloat16),
            jax.ShapeDtypeStruct((rows, outs - DH), jnp.bfloat16),
        ],
        compiler_params=pltpu.CompilerParams(vmem_limit_bytes=48 * 1024 * 1024),
        cost_estimate=pl.CostEstimate(
            flops=2 * rows * width * outs + 10 * rows * width,
            transcendentals=rows,
            bytes_accessed=2 * rows * width + 2 * width * outs + 2 * rows * outs,
        ),
    )(rows_t, mod_cols, weights_t)


def attention_kernel(q_ref, kv_ref, o_ref):
    keys = kv_ref[:, :DH]
    values = kv_ref[:, DH:]
    scores = lax.dot_general(
        q_ref[...], keys, (((1,), (1,)), ((), ())), preferred_element_type=jnp.float32
    ) * (DH ** (-0.5))
    shifted = jnp.exp(scores - jnp.max(scores, axis=1, keepdims=True))
    row_sum = jnp.sum(shifted, axis=1, keepdims=True)
    numer = jnp.dot(shifted.astype(jnp.bfloat16), values, preferred_element_type=jnp.float32)
    o_ref[...] = (numer / row_sum).astype(o_ref.dtype)


def attention(queries, key_values, block=256):
    rows = queries.shape[0]
    count = key_values.shape[0]
    return pl.pallas_call(
        attention_kernel,
        grid=(rows // block,),
        in_specs=[
            pl.BlockSpec((block, DH), lambda i: (i, 0)),
            pl.BlockSpec((count, 2 * DH), lambda i: (0, 0)),
        ],
        out_specs=pl.BlockSpec((block, DH), lambda i: (i, 0)),
        out_shape=jax.ShapeDtypeStruct((rows, DH), jnp.bfloat16),
        compiler_params=pltpu.CompilerParams(vmem_limit_bytes=56 * 1024 * 1024),
        cost_estimate=pl.CostEstimate(
            flops=4 * rows * count * DH,
            transcendentals=rows * count,
            bytes_accessed=4 * rows * DH + 4 * count * DH,
        ),
    )(queries, key_values)


def body(tokens, defect_mask, timestep, mask_embed, mod_weight, w_qkv, w_out):
    tok_rows = tokens.shape[0]
    residual_in = (
        tokens.astype(jnp.float32)
        + defect_mask.astype(jnp.float32)[:, None] * mask_embed.astype(jnp.float32)[None, :]
    ).astype(jnp.bfloat16)
    tok_count = lax.axis_size("tok")
    w_copies = jnp.broadcast_to(w_qkv[None], (tok_count,) + w_qkv.shape)
    w_full = lax.all_to_all(w_copies, "tok", split_axis=0, concat_axis=0, tiled=True)
    w_full = w_full.reshape((tok_count * w_qkv.shape[0],) + w_qkv.shape[1:])
    half_width = TEMB // 2
    frequency = jnp.exp(-math.log(10000.0) * jnp.arange(half_width, dtype=jnp.float32) / half_width)
    angles = timestep.astype(jnp.float32)[0] * frequency
    embedding = jnp.concatenate([jnp.cos(angles), jnp.sin(angles)])
    modulation = jnp.einsum(
        "e,ecf->cf",
        jax.nn.silu(embedding),
        mod_weight.astype(jnp.float32),
        precision=lax.Precision.HIGHEST,
    ).astype(jnp.bfloat16)
    residual_full = lax.all_gather(residual_in, "wid", axis=1, tiled=True)
    wid_count = lax.axis_size("wid")
    mod_copies = jnp.broadcast_to(modulation[None, :2], (wid_count, 2, modulation.shape[1]))
    mod_parts = lax.all_to_all(mod_copies, "wid", split_axis=0, concat_axis=0, tiled=True)
    shift_scale = jnp.transpose(mod_parts, (1, 0, 2)).reshape(2, wid_count * modulation.shape[1])
    weights_t = w_full.reshape(w_full.shape[0], 3 * DH).T
    qkv = tuple(project(residual_full.T, shift_scale.T, weights_t))
    w_late, qkv = lax.optimization_barrier((w_out, qkv))
    w_cols = lax.all_to_all(w_late, "wid", split_axis=1, concat_axis=0, tiled=True)
    queries, key_rows = qkv
    key_values = lax.all_gather(key_rows, "tok", axis=0, tiled=True)
    w_cols, key_values = lax.optimization_barrier((w_cols, key_values))
    attended = attention(queries, key_values)
    heads = lax.all_gather(attended, "wid", axis=0, tiled=False)
    projected = jnp.einsum(
        "htd,hdc->tc",
        heads,
        w_cols.reshape(heads.shape[0], DH, w_cols.shape[1]),
        preferred_element_type=jnp.float32,
    )
    return (
        residual_in.astype(jnp.float32) + modulation[2].astype(jnp.float32)[None, :] * projected
    ).astype(jnp.bfloat16)


def solution(mesh):
    return jax.shard_map(
        body,
        mesh=mesh,
        in_specs=(
            P("tok", "wid"),
            P("tok"),
            P(),
            P("wid"),
            P(None, None, "wid"),
            P("tok", None, "wid"),
            P("wid", None),
        ),
        out_specs=P("tok", "wid"),
        check_vma=False,
    )
```

```python
import math

import jax
import jax.numpy as jnp
from jax import lax
from jax.experimental import pallas as pl
from jax.experimental.pallas import tpu as pltpu
from jax.sharding import PartitionSpec as P

D = 3072
DH = 128
TEMB = 256


def finish_rows(values, row_mean, row_var, shift_row, scale_row):
    normal = (values - row_mean) * lax.rsqrt(row_var + 1e-06)
    return (normal * (1.0 + scale_row.astype(jnp.float32)) + shift_row.astype(jnp.float32)).astype(
        jnp.bfloat16
    )


def project_kernel(x_ref, mod_ref, w_ref, q_ref, kv_ref):
    values = x_ref[...].astype(jnp.float32)
    width = values.shape[0]
    row_mean = jnp.sum(values, axis=0, keepdims=True) / width
    row_var = jnp.sum(values * values, axis=0, keepdims=True) / width - row_mean * row_mean
    normal = (values - row_mean) * lax.rsqrt(row_var + 1e-06)
    shift_col = mod_ref[:, 0:1].astype(jnp.float32)
    scale_col = mod_ref[:, 1:2].astype(jnp.float32)
    normed = (normal * (1.0 + scale_col) + shift_col).astype(jnp.bfloat16)
    qkv_t = jnp.dot(w_ref[...], normed, preferred_element_type=jnp.float32)
    qkv = jnp.transpose(qkv_t).astype(jnp.bfloat16)
    q_ref[...] = qkv[:, :DH]
    kv_ref[...] = qkv[:, DH:]


def project(rows_t, mod_cols, weights_t, block=256):
    width, rows = rows_t.shape
    outs = weights_t.shape[0]
    return pl.pallas_call(
        project_kernel,
        grid=(rows // block,),
        in_specs=[
            pl.BlockSpec((width, block), lambda i: (0, i)),
            pl.BlockSpec(mod_cols.shape, lambda i: (0, 0)),
            pl.BlockSpec(weights_t.shape, lambda i: (0, 0)),
        ],
        out_specs=[
            pl.BlockSpec((block, DH), lambda i: (i, 0)),
            pl.BlockSpec((block, outs - DH), lambda i: (i, 0)),
        ],
        out_shape=[
            jax.ShapeDtypeStruct((rows, DH), jnp.bfloat16),
            jax.ShapeDtypeStruct((rows, outs - DH), jnp.bfloat16),
        ],
        compiler_params=pltpu.CompilerParams(vmem_limit_bytes=48 * 1024 * 1024),
        cost_estimate=pl.CostEstimate(
            flops=2 * rows * width * outs + 10 * rows * width,
            transcendentals=rows,
            bytes_accessed=2 * rows * width + 2 * width * outs + 2 * rows * outs,
        ),
    )(rows_t, mod_cols, weights_t)


def attention_kernel(q_ref, kv_ref, o_ref):
    keys = kv_ref[:, :DH]
    values = kv_ref[:, DH:]
    scores = lax.dot_general(
        q_ref[...], keys, (((1,), (1,)), ((), ())), preferred_element_type=jnp.float32
    ) * (DH ** (-0.5))
    shifted = jnp.exp(scores - jnp.max(scores, axis=1, keepdims=True))
    row_sum = jnp.sum(shifted, axis=1, keepdims=True)
    numer = jnp.dot(shifted.astype(jnp.bfloat16), values, preferred_element_type=jnp.float32)
    o_ref[...] = (numer / row_sum).astype(o_ref.dtype)


def attention(queries, key_values, block=256):
    rows = queries.shape[0]
    count = key_values.shape[0]
    return pl.pallas_call(
        attention_kernel,
        grid=(rows // block,),
        in_specs=[
            pl.BlockSpec((block, DH), lambda i: (i, 0)),
            pl.BlockSpec((count, 2 * DH), lambda i: (0, 0)),
        ],
        out_specs=pl.BlockSpec((block, DH), lambda i: (i, 0)),
        out_shape=jax.ShapeDtypeStruct((rows, DH), jnp.bfloat16),
        compiler_params=pltpu.CompilerParams(vmem_limit_bytes=56 * 1024 * 1024),
        cost_estimate=pl.CostEstimate(
            flops=4 * rows * count * DH,
            transcendentals=rows * count,
            bytes_accessed=4 * rows * DH + 4 * count * DH,
        ),
    )(queries, key_values)


def output_kernel(h_ref, w_ref, r_ref, g_ref, o_ref):
    total = jnp.zeros(o_ref.shape, jnp.float32)
    for head in range(h_ref.shape[0]):
        total = total + jnp.dot(h_ref[head], w_ref[head], preferred_element_type=jnp.float32)
    o_ref[...] = (r_ref[...].astype(jnp.float32) + g_ref[...] * total).astype(o_ref.dtype)


def output_projection(heads, w_heads, residual, gate, block=256):
    count, rows, _ = heads.shape
    cols = w_heads.shape[2]
    return pl.pallas_call(
        output_kernel,
        grid=(rows // block,),
        in_specs=[
            pl.BlockSpec((count, block, DH), lambda i: (0, i, 0)),
            pl.BlockSpec(w_heads.shape, lambda i: (0, 0, 0)),
            pl.BlockSpec((block, cols), lambda i: (i, 0)),
            pl.BlockSpec(gate.shape, lambda i: (0, 0)),
        ],
        out_specs=pl.BlockSpec((block, cols), lambda i: (i, 0)),
        out_shape=jax.ShapeDtypeStruct((rows, cols), jnp.bfloat16),
        cost_estimate=pl.CostEstimate(
            flops=2 * count * rows * DH * cols,
            transcendentals=0,
            bytes_accessed=2 * heads.size + 2 * w_heads.size + 4 * rows * cols,
        ),
    )(heads, w_heads, residual, gate)


def body(tokens, defect_mask, timestep, mask_embed, mod_weight, w_qkv, w_out):
    tok_rows = tokens.shape[0]
    residual_in = (
        tokens.astype(jnp.float32)
        + defect_mask.astype(jnp.float32)[:, None] * mask_embed.astype(jnp.float32)[None, :]
    ).astype(jnp.bfloat16)
    tok_count = lax.axis_size("tok")
    w_copies = jnp.broadcast_to(w_qkv[None], (tok_count,) + w_qkv.shape)
    w_full = lax.all_to_all(w_copies, "tok", split_axis=0, concat_axis=0, tiled=True)
    w_full = w_full.reshape((tok_count * w_qkv.shape[0],) + w_qkv.shape[1:])
    half_width = TEMB // 2
    frequency = jnp.exp(-math.log(10000.0) * jnp.arange(half_width, dtype=jnp.float32) / half_width)
    angles = timestep.astype(jnp.float32)[0] * frequency
    embedding = jnp.concatenate([jnp.cos(angles), jnp.sin(angles)])
    modulation = jnp.einsum(
        "e,ecf->cf",
        jax.nn.silu(embedding),
        mod_weight.astype(jnp.float32),
        precision=lax.Precision.HIGHEST,
    ).astype(jnp.bfloat16)
    residual_full = lax.all_gather(residual_in, "wid", axis=1, tiled=True)
    wid_count = lax.axis_size("wid")
    mod_copies = jnp.broadcast_to(modulation[None, :2], (wid_count, 2, modulation.shape[1]))
    mod_parts = lax.all_to_all(mod_copies, "wid", split_axis=0, concat_axis=0, tiled=True)
    shift_scale = jnp.transpose(mod_parts, (1, 0, 2)).reshape(2, wid_count * modulation.shape[1])
    weights_t = w_full.reshape(w_full.shape[0], 3 * DH).T
    qkv = tuple(project(residual_full.T, shift_scale.T, weights_t))
    w_late, qkv = lax.optimization_barrier((w_out, qkv))
    w_cols = lax.all_to_all(w_late, "wid", split_axis=1, concat_axis=0, tiled=True)
    queries, key_rows = qkv
    key_values = lax.all_gather(key_rows, "tok", axis=0, tiled=True)
    w_cols, key_values = lax.optimization_barrier((w_cols, key_values))
    attended = attention(queries, key_values)
    heads = lax.all_gather(attended, "wid", axis=0, tiled=False)
    return output_projection(
        heads,
        w_cols.reshape(heads.shape[0], DH, w_cols.shape[1]),
        residual_in,
        modulation[2:3].astype(jnp.float32),
    )


def solution(mesh):
    return jax.shard_map(
        body,
        mesh=mesh,
        in_specs=(
            P("tok", "wid"),
            P("tok"),
            P(),
            P("wid"),
            P(None, None, "wid"),
            P("tok", None, "wid"),
            P("wid", None),
        ),
        out_specs=P("tok", "wid"),
        check_vma=False,
    )
```

```python
import math

import jax
import jax.numpy as jnp
from jax import lax
from jax.experimental import pallas as pl
from jax.experimental.pallas import tpu as pltpu
from jax.sharding import PartitionSpec as P

D = 3072
DH = 128
TEMB = 256


def finish_rows(values, row_mean, row_var, shift_row, scale_row):
    normal = (values - row_mean) * lax.rsqrt(row_var + 1e-06)
    return (normal * (1.0 + scale_row.astype(jnp.float32)) + shift_row.astype(jnp.float32)).astype(
        jnp.bfloat16
    )


def project_kernel(x_ref, mod_ref, w_ref, q_init, kv_init, q_ref, kv_ref):
    values = x_ref[...].astype(jnp.float32)
    width = values.shape[0]
    row_mean = jnp.sum(values, axis=0, keepdims=True) / width
    row_var = jnp.sum(values * values, axis=0, keepdims=True) / width - row_mean * row_mean
    normal = (values - row_mean) * lax.rsqrt(row_var + 1e-06)
    shift_col = mod_ref[:, 0:1].astype(jnp.float32)
    scale_col = mod_ref[:, 1:2].astype(jnp.float32)
    normed = (normal * (1.0 + scale_col) + shift_col).astype(jnp.bfloat16)
    qkv_t = jnp.dot(w_ref[...], normed, preferred_element_type=jnp.float32)
    qkv = jnp.transpose(qkv_t).astype(jnp.bfloat16)
    q_ref[...] = qkv[:, :DH]
    kv_ref[...] = qkv[:, DH:]


def project(rows_t, mod_cols, weights_t, block=256):
    width, rows = rows_t.shape
    outs = weights_t.shape[0]
    return pl.pallas_call(
        project_kernel,
        grid=(rows // block,),
        in_specs=[
            pl.BlockSpec((width, block), lambda i: (0, i)),
            pl.BlockSpec(mod_cols.shape, lambda i: (0, 0)),
            pl.BlockSpec(weights_t.shape, lambda i: (0, 0)),
            pl.BlockSpec(memory_space=pltpu.HBM),
            pl.BlockSpec(memory_space=pltpu.HBM),
        ],
        out_specs=[
            pl.BlockSpec((block, DH), lambda i: (i, 0)),
            pl.BlockSpec((block, outs - DH), lambda i: (i, 0)),
        ],
        out_shape=[
            jax.ShapeDtypeStruct((rows, DH), jnp.bfloat16),
            jax.ShapeDtypeStruct((rows, outs - DH), jnp.bfloat16),
        ],
        compiler_params=pltpu.CompilerParams(vmem_limit_bytes=48 * 1024 * 1024),
        cost_estimate=pl.CostEstimate(
            flops=2 * rows * width * outs + 10 * rows * width,
            transcendentals=rows,
            bytes_accessed=2 * rows * width + 2 * width * outs + 2 * rows * outs,
        ),
        input_output_aliases={3: 0, 4: 1},
    )(
        rows_t,
        mod_cols,
        weights_t,
        pltpu.with_memory_space_constraint(jnp.zeros((rows, DH), jnp.bfloat16), pltpu.HBM),
        pltpu.with_memory_space_constraint(jnp.zeros((rows, outs - DH), jnp.bfloat16), pltpu.HBM),
    )


def attention_kernel(q_ref, kv_ref, o_ref):
    keys = kv_ref[:, :DH]
    values = kv_ref[:, DH:]
    scores = lax.dot_general(
        q_ref[...], keys, (((1,), (1,)), ((), ())), preferred_element_type=jnp.float32
    ) * (DH ** (-0.5))
    shifted = jnp.exp(scores - jnp.max(scores, axis=1, keepdims=True))
    row_sum = jnp.sum(shifted, axis=1, keepdims=True)
    numer = jnp.dot(shifted.astype(jnp.bfloat16), values, preferred_element_type=jnp.float32)
    o_ref[...] = (numer / row_sum).astype(o_ref.dtype)


def attention(queries, key_values, block=256):
    rows = queries.shape[0]
    count = key_values.shape[0]
    return pl.pallas_call(
        attention_kernel,
        grid=(rows // block,),
        in_specs=[
            pl.BlockSpec((block, DH), lambda i: (i, 0)),
            pl.BlockSpec((count, 2 * DH), lambda i: (0, 0)),
        ],
        out_specs=pl.BlockSpec((block, DH), lambda i: (i, 0)),
        out_shape=jax.ShapeDtypeStruct((rows, DH), jnp.bfloat16),
        compiler_params=pltpu.CompilerParams(vmem_limit_bytes=56 * 1024 * 1024),
        cost_estimate=pl.CostEstimate(
            flops=4 * rows * count * DH,
            transcendentals=rows * count,
            bytes_accessed=4 * rows * DH + 4 * count * DH,
        ),
    )(queries, key_values)


def body(tokens, defect_mask, timestep, mask_embed, mod_weight, w_qkv, w_out):
    tok_rows = tokens.shape[0]
    residual_in = (
        tokens.astype(jnp.float32)
        + defect_mask.astype(jnp.float32)[:, None] * mask_embed.astype(jnp.float32)[None, :]
    ).astype(jnp.bfloat16)
    tok_count = lax.axis_size("tok")
    w_copies = jnp.broadcast_to(w_qkv[None], (tok_count,) + w_qkv.shape)
    w_full = lax.all_to_all(w_copies, "tok", split_axis=0, concat_axis=0, tiled=True)
    w_full = w_full.reshape((tok_count * w_qkv.shape[0],) + w_qkv.shape[1:])
    half_width = TEMB // 2
    frequency = jnp.exp(-math.log(10000.0) * jnp.arange(half_width, dtype=jnp.float32) / half_width)
    angles = timestep.astype(jnp.float32)[0] * frequency
    embedding = jnp.concatenate([jnp.cos(angles), jnp.sin(angles)])
    modulation = jnp.einsum(
        "e,ecf->cf",
        jax.nn.silu(embedding),
        mod_weight.astype(jnp.float32),
        precision=lax.Precision.HIGHEST,
    ).astype(jnp.bfloat16)
    residual_full = lax.all_gather(residual_in, "wid", axis=1, tiled=True)
    wid_count = lax.axis_size("wid")
    mod_copies = jnp.broadcast_to(modulation[None, :2], (wid_count, 2, modulation.shape[1]))
    mod_parts = lax.all_to_all(mod_copies, "wid", split_axis=0, concat_axis=0, tiled=True)
    shift_scale = jnp.transpose(mod_parts, (1, 0, 2)).reshape(2, wid_count * modulation.shape[1])
    weights_t = w_full.reshape(w_full.shape[0], 3 * DH).T
    qkv = tuple(project(residual_full.T, shift_scale.T, weights_t))
    w_late, qkv = lax.optimization_barrier((w_out, qkv))
    w_cols = lax.all_to_all(w_late, "wid", split_axis=1, concat_axis=0, tiled=True)
    queries, key_rows = qkv
    key_values = lax.all_gather(key_rows, "tok", axis=0, tiled=True)
    w_cols, key_values = lax.optimization_barrier((w_cols, key_values))
    attended = attention(queries, key_values)
    heads = lax.all_gather(attended, "wid", axis=0, tiled=False)
    projected = jnp.einsum(
        "htd,hdc->tc",
        heads,
        w_cols.reshape(heads.shape[0], DH, w_cols.shape[1]),
        preferred_element_type=jnp.float32,
    )
    return (
        residual_in.astype(jnp.float32) + modulation[2].astype(jnp.float32)[None, :] * projected
    ).astype(jnp.bfloat16)


def solution(mesh):
    return jax.shard_map(
        body,
        mesh=mesh,
        in_specs=(
            P("tok", "wid"),
            P("tok"),
            P(),
            P("wid"),
            P(None, None, "wid"),
            P("tok", None, "wid"),
            P("wid", None),
        ),
        out_specs=P("tok", "wid"),
        check_vma=False,
    )
```

```python
import math

import jax
import jax.numpy as jnp
from jax import lax
from jax.experimental import pallas as pl
from jax.experimental.pallas import tpu as pltpu
from jax.sharding import PartitionSpec as P

D = 3072
DH = 128
TEMB = 256


def finish_rows(values, row_mean, row_var, shift_row, scale_row):
    normal = (values - row_mean) * lax.rsqrt(row_var + 1e-06)
    return (normal * (1.0 + scale_row.astype(jnp.float32)) + shift_row.astype(jnp.float32)).astype(
        jnp.bfloat16
    )


def project_kernel(x_ref, mod_ref, w_ref, q_init, kv_init, q_ref, kv_ref):
    values = x_ref[...].astype(jnp.float32)
    width = values.shape[0]
    row_mean = jnp.sum(values, axis=0, keepdims=True) / width
    row_var = jnp.sum(values * values, axis=0, keepdims=True) / width - row_mean * row_mean
    normal = (values - row_mean) * lax.rsqrt(row_var + 1e-06)
    shift_col = mod_ref[:, 0:1].astype(jnp.float32)
    scale_col = mod_ref[:, 1:2].astype(jnp.float32)
    normed = (normal * (1.0 + scale_col) + shift_col).astype(jnp.bfloat16)
    qkv_t = jnp.dot(w_ref[...], normed, preferred_element_type=jnp.float32)
    qkv = jnp.transpose(qkv_t).astype(jnp.bfloat16)
    q_ref[...] = qkv[:, :DH]
    kv_ref[...] = qkv[:, DH:]


def project(rows_t, mod_cols, weights_t, q_init, kv_init, block=256):
    width, rows = rows_t.shape
    outs = weights_t.shape[0]
    return pl.pallas_call(
        project_kernel,
        grid=(rows // block,),
        in_specs=[
            pl.BlockSpec((width, block), lambda i: (0, i)),
            pl.BlockSpec(mod_cols.shape, lambda i: (0, 0)),
            pl.BlockSpec(weights_t.shape, lambda i: (0, 0)),
            pl.BlockSpec(memory_space=pltpu.HBM),
            pl.BlockSpec(memory_space=pltpu.HBM),
        ],
        out_specs=[
            pl.BlockSpec((block, DH), lambda i: (i, 0)),
            pl.BlockSpec((block, outs - DH), lambda i: (i, 0)),
        ],
        out_shape=[
            jax.ShapeDtypeStruct((rows, DH), jnp.bfloat16),
            jax.ShapeDtypeStruct((rows, outs - DH), jnp.bfloat16),
        ],
        compiler_params=pltpu.CompilerParams(vmem_limit_bytes=48 * 1024 * 1024),
        cost_estimate=pl.CostEstimate(
            flops=2 * rows * width * outs + 10 * rows * width,
            transcendentals=rows,
            bytes_accessed=2 * rows * width + 2 * width * outs + 2 * rows * outs,
        ),
        input_output_aliases={3: 0, 4: 1},
    )(
        rows_t,
        mod_cols,
        weights_t,
        pltpu.with_memory_space_constraint(q_init, pltpu.HBM),
        pltpu.with_memory_space_constraint(kv_init, pltpu.HBM),
    )


def attention_kernel(q_ref, kv_ref, o_ref):
    keys = kv_ref[:, :DH]
    values = kv_ref[:, DH:]
    scores = lax.dot_general(
        q_ref[...], keys, (((1,), (1,)), ((), ())), preferred_element_type=jnp.float32
    ) * (DH ** (-0.5))
    shifted = jnp.exp(scores - jnp.max(scores, axis=1, keepdims=True))
    row_sum = jnp.sum(shifted, axis=1, keepdims=True)
    numer = jnp.dot(shifted.astype(jnp.bfloat16), values, preferred_element_type=jnp.float32)
    o_ref[...] = (numer / row_sum).astype(o_ref.dtype)


def attention(queries, key_values, block=256):
    rows = queries.shape[0]
    count = key_values.shape[0]
    return pl.pallas_call(
        attention_kernel,
        grid=(rows // block,),
        in_specs=[
            pl.BlockSpec((block, DH), lambda i: (i, 0)),
            pl.BlockSpec((count, 2 * DH), lambda i: (0, 0)),
        ],
        out_specs=pl.BlockSpec((block, DH), lambda i: (i, 0)),
        out_shape=jax.ShapeDtypeStruct((rows, DH), jnp.bfloat16),
        compiler_params=pltpu.CompilerParams(vmem_limit_bytes=56 * 1024 * 1024),
        cost_estimate=pl.CostEstimate(
            flops=4 * rows * count * DH,
            transcendentals=rows * count,
            bytes_accessed=4 * rows * DH + 4 * count * DH,
        ),
    )(queries, key_values)


def body(tokens, defect_mask, timestep, mask_embed, mod_weight, w_qkv, w_out):
    tok_rows = tokens.shape[0]
    residual_in = (
        tokens.astype(jnp.float32)
        + defect_mask.astype(jnp.float32)[:, None] * mask_embed.astype(jnp.float32)[None, :]
    ).astype(jnp.bfloat16)
    tok_count = lax.axis_size("tok")
    w_copies = jnp.broadcast_to(w_qkv[None], (tok_count,) + w_qkv.shape)
    w_full = lax.all_to_all(w_copies, "tok", split_axis=0, concat_axis=0, tiled=True)
    w_full = w_full.reshape((tok_count * w_qkv.shape[0],) + w_qkv.shape[1:])
    half_width = TEMB // 2
    frequency = jnp.exp(-math.log(10000.0) * jnp.arange(half_width, dtype=jnp.float32) / half_width)
    angles = timestep.astype(jnp.float32)[0] * frequency
    embedding = jnp.concatenate([jnp.cos(angles), jnp.sin(angles)])
    modulation = jnp.einsum(
        "e,ecf->cf",
        jax.nn.silu(embedding),
        mod_weight.astype(jnp.float32),
        precision=lax.Precision.HIGHEST,
    ).astype(jnp.bfloat16)
    residual_full = lax.all_gather(residual_in, "wid", axis=1, tiled=True)
    wid_count = lax.axis_size("wid")
    mod_copies = jnp.broadcast_to(modulation[None, :2], (wid_count, 2, modulation.shape[1]))
    mod_parts = lax.all_to_all(mod_copies, "wid", split_axis=0, concat_axis=0, tiled=True)
    shift_scale = jnp.transpose(mod_parts, (1, 0, 2)).reshape(2, wid_count * modulation.shape[1])
    q_init = residual_in[:, :DH]
    kv_init = jnp.concatenate([q_init, q_init], axis=1)
    q_init, kv_init, w_full = lax.optimization_barrier((q_init, kv_init, w_full))
    weights_t = w_full.reshape(w_full.shape[0], 3 * DH).T
    qkv = tuple(project(residual_full.T, shift_scale.T, weights_t, q_init, kv_init))
    w_late, qkv = lax.optimization_barrier((w_out, qkv))
    w_cols = lax.all_to_all(w_late, "wid", split_axis=1, concat_axis=0, tiled=True)
    queries, key_rows = qkv
    key_values = lax.all_gather(key_rows, "tok", axis=0, tiled=True)
    w_cols, key_values = lax.optimization_barrier((w_cols, key_values))
    attended = attention(queries, key_values)
    heads = lax.all_gather(attended, "wid", axis=0, tiled=False)
    projected = jnp.einsum(
        "htd,hdc->tc",
        heads,
        w_cols.reshape(heads.shape[0], DH, w_cols.shape[1]),
        preferred_element_type=jnp.float32,
    )
    return (
        residual_in.astype(jnp.float32) + modulation[2].astype(jnp.float32)[None, :] * projected
    ).astype(jnp.bfloat16)


def solution(mesh):
    return jax.shard_map(
        body,
        mesh=mesh,
        in_specs=(
            P("tok", "wid"),
            P("tok"),
            P(),
            P("wid"),
            P(None, None, "wid"),
            P("tok", None, "wid"),
            P("wid", None),
        ),
        out_specs=P("tok", "wid"),
        check_vma=False,
    )
```

```python
import math

import jax
import jax.numpy as jnp
from jax import lax
from jax.experimental import pallas as pl
from jax.experimental.pallas import tpu as pltpu
from jax.sharding import PartitionSpec as P

D = 3072
DH = 128
TEMB = 256


def finish_rows(values, row_mean, row_var, shift_row, scale_row):
    normal = (values - row_mean) * lax.rsqrt(row_var + 1e-06)
    return (normal * (1.0 + scale_row.astype(jnp.float32)) + shift_row.astype(jnp.float32)).astype(
        jnp.bfloat16
    )


def project_kernel(x_ref, mod_ref, w_ref, q_init, kv_init, q_ref, kv_ref):
    values = x_ref[...].astype(jnp.float32)
    width = values.shape[0]
    row_mean = jnp.sum(values, axis=0, keepdims=True) / width
    row_var = jnp.sum(values * values, axis=0, keepdims=True) / width - row_mean * row_mean
    normal = (values - row_mean) * lax.rsqrt(row_var + 1e-06)
    shift_col = mod_ref[:, 0:1].astype(jnp.float32)
    scale_col = mod_ref[:, 1:2].astype(jnp.float32)
    normed = (normal * (1.0 + scale_col) + shift_col).astype(jnp.bfloat16)
    qkv_t = jnp.dot(w_ref[...], normed, preferred_element_type=jnp.float32)
    qkv = jnp.transpose(qkv_t).astype(jnp.bfloat16)
    q_ref[...] = qkv[:, :DH]
    kv_ref[...] = qkv[:, DH:]


def project(rows_t, mod_cols, weights_t, q_init, kv_init, block=256):
    width, rows = rows_t.shape
    outs = weights_t.shape[0]
    return pl.pallas_call(
        project_kernel,
        grid=(rows // block,),
        in_specs=[
            pl.BlockSpec((width, block), lambda i: (0, i)),
            pl.BlockSpec(mod_cols.shape, lambda i: (0, 0)),
            pl.BlockSpec(weights_t.shape, lambda i: (0, 0)),
            pl.BlockSpec(memory_space=pltpu.HBM),
            pl.BlockSpec(memory_space=pltpu.HBM),
        ],
        out_specs=[
            pl.BlockSpec((block, DH), lambda i: (i, 0)),
            pl.BlockSpec((block, outs - DH), lambda i: (i, 0)),
        ],
        out_shape=[
            jax.ShapeDtypeStruct((rows, DH), jnp.bfloat16),
            jax.ShapeDtypeStruct((rows, outs - DH), jnp.bfloat16),
        ],
        compiler_params=pltpu.CompilerParams(vmem_limit_bytes=48 * 1024 * 1024),
        cost_estimate=pl.CostEstimate(
            flops=2 * rows * width * outs + 10 * rows * width,
            transcendentals=rows,
            bytes_accessed=2 * rows * width + 2 * width * outs + 2 * rows * outs,
        ),
        input_output_aliases={3: 0, 4: 1},
    )(
        rows_t,
        mod_cols,
        weights_t,
        pltpu.with_memory_space_constraint(q_init, pltpu.HBM),
        pltpu.with_memory_space_constraint(kv_init, pltpu.HBM),
    )


def attention_kernel(q_ref, kv_ref, o_ref):
    keys = kv_ref[:, :DH]
    values = kv_ref[:, DH:]
    scores = lax.dot_general(
        q_ref[...], keys, (((1,), (1,)), ((), ())), preferred_element_type=jnp.float32
    ) * (DH ** (-0.5))
    shifted = jnp.exp(scores - jnp.max(scores, axis=1, keepdims=True))
    row_sum = jnp.sum(shifted, axis=1, keepdims=True)
    numer = jnp.dot(shifted.astype(jnp.bfloat16), values, preferred_element_type=jnp.float32)
    o_ref[...] = (numer / row_sum).astype(o_ref.dtype)


def attention(queries, key_values, block=256):
    rows = queries.shape[0]
    count = key_values.shape[0]
    return pl.pallas_call(
        attention_kernel,
        grid=(rows // block,),
        in_specs=[
            pl.BlockSpec((block, DH), lambda i: (i, 0)),
            pl.BlockSpec((count, 2 * DH), lambda i: (0, 0)),
        ],
        out_specs=pl.BlockSpec((block, DH), lambda i: (i, 0)),
        out_shape=jax.ShapeDtypeStruct((rows, DH), jnp.bfloat16),
        compiler_params=pltpu.CompilerParams(vmem_limit_bytes=56 * 1024 * 1024),
        cost_estimate=pl.CostEstimate(
            flops=4 * rows * count * DH,
            transcendentals=rows * count,
            bytes_accessed=4 * rows * DH + 4 * count * DH,
        ),
    )(queries, key_values)


def body(tokens, defect_mask, timestep, mask_embed, mod_weight, w_qkv, w_out):
    tok_rows = tokens.shape[0]
    residual_in = (
        tokens.astype(jnp.float32)
        + defect_mask.astype(jnp.float32)[:, None] * mask_embed.astype(jnp.float32)[None, :]
    ).astype(jnp.bfloat16)
    tok_count = lax.axis_size("tok")
    w_copies = jnp.broadcast_to(w_qkv[None], (tok_count,) + w_qkv.shape)
    w_full = lax.all_to_all(w_copies, "tok", split_axis=0, concat_axis=0, tiled=True)
    w_full = w_full.reshape((tok_count * w_qkv.shape[0],) + w_qkv.shape[1:])
    half_width = TEMB // 2
    frequency = jnp.exp(-math.log(10000.0) * jnp.arange(half_width, dtype=jnp.float32) / half_width)
    angles = timestep.astype(jnp.float32)[0] * frequency
    embedding = jnp.concatenate([jnp.cos(angles), jnp.sin(angles)])
    modulation = jnp.einsum(
        "e,ecf->cf",
        jax.nn.silu(embedding),
        mod_weight.astype(jnp.float32),
        precision=lax.Precision.HIGHEST,
    ).astype(jnp.bfloat16)
    residual_full = lax.all_gather(residual_in, "wid", axis=1, tiled=True)
    wid_count = lax.axis_size("wid")
    mod_copies = jnp.broadcast_to(modulation[None, :2], (wid_count, 2, modulation.shape[1]))
    mod_parts = lax.all_to_all(mod_copies, "wid", split_axis=0, concat_axis=0, tiled=True)
    shift_scale = jnp.transpose(mod_parts, (1, 0, 2)).reshape(2, wid_count * modulation.shape[1])
    w_rows = w_full.reshape(w_full.shape[0], 3 * DH)[:tok_rows]
    q_init = w_rows[:, :DH]
    kv_init = w_rows[:, DH:]
    q_init, kv_init, w_full = lax.optimization_barrier((q_init, kv_init, w_full))
    weights_t = w_full.reshape(w_full.shape[0], 3 * DH).T
    qkv = tuple(project(residual_full.T, shift_scale.T, weights_t, q_init, kv_init))
    w_late, qkv = lax.optimization_barrier((w_out, qkv))
    w_cols = lax.all_to_all(w_late, "wid", split_axis=1, concat_axis=0, tiled=True)
    queries, key_rows = qkv
    key_values = lax.all_gather(key_rows, "tok", axis=0, tiled=True)
    w_cols, key_values = lax.optimization_barrier((w_cols, key_values))
    attended = attention(queries, key_values)
    heads = lax.all_gather(attended, "wid", axis=0, tiled=False)
    projected = jnp.einsum(
        "htd,hdc->tc",
        heads,
        w_cols.reshape(heads.shape[0], DH, w_cols.shape[1]),
        preferred_element_type=jnp.float32,
    )
    return (
        residual_in.astype(jnp.float32) + modulation[2].astype(jnp.float32)[None, :] * projected
    ).astype(jnp.bfloat16)


def solution(mesh):
    return jax.shard_map(
        body,
        mesh=mesh,
        in_specs=(
            P("tok", "wid"),
            P("tok"),
            P(),
            P("wid"),
            P(None, None, "wid"),
            P("tok", None, "wid"),
            P("wid", None),
        ),
        out_specs=P("tok", "wid"),
        check_vma=False,
    )
```

```python
import math

import jax
import jax.numpy as jnp
from jax import lax
from jax.experimental import pallas as pl
from jax.experimental.pallas import tpu as pltpu
from jax.sharding import PartitionSpec as P

D = 3072
DH = 128
TEMB = 256


def finish_rows(values, row_mean, row_var, shift_row, scale_row):
    normal = (values - row_mean) * lax.rsqrt(row_var + 1e-06)
    return (normal * (1.0 + scale_row.astype(jnp.float32)) + shift_row.astype(jnp.float32)).astype(
        jnp.bfloat16
    )


def project_kernel(x_ref, mod_ref, w_ref, q_init, kv_init, q_ref, kv_ref):
    values = x_ref[...].astype(jnp.float32)
    width = values.shape[0]
    row_mean = jnp.sum(values, axis=0, keepdims=True) / width
    row_var = jnp.sum(values * values, axis=0, keepdims=True) / width - row_mean * row_mean
    normal = (values - row_mean) * lax.rsqrt(row_var + 1e-06)
    shift_col = mod_ref[:, 0:1].astype(jnp.float32)
    scale_col = mod_ref[:, 1:2].astype(jnp.float32)
    normed = (normal * (1.0 + scale_col) + shift_col).astype(jnp.bfloat16)
    qkv_t = jnp.dot(w_ref[...], normed, preferred_element_type=jnp.float32)
    qkv = jnp.transpose(qkv_t).astype(jnp.bfloat16)
    q_ref[...] = qkv[:, :DH]
    kv_ref[...] = qkv[:, DH:]


def project(rows_t, mod_cols, weights_t, q_init, kv_init, block=256):
    width, rows = rows_t.shape
    outs = weights_t.shape[0]
    return pl.pallas_call(
        project_kernel,
        grid=(rows // block,),
        in_specs=[
            pl.BlockSpec((width, block), lambda i: (0, i)),
            pl.BlockSpec(mod_cols.shape, lambda i: (0, 0)),
            pl.BlockSpec(weights_t.shape, lambda i: (0, 0)),
            pl.BlockSpec(memory_space=pltpu.HBM),
            pl.BlockSpec(memory_space=pltpu.HBM),
        ],
        out_specs=[
            pl.BlockSpec((block, DH), lambda i: (i, 0)),
            pl.BlockSpec((block, outs - DH), lambda i: (i, 0)),
        ],
        out_shape=[
            jax.ShapeDtypeStruct((rows, DH), jnp.bfloat16),
            jax.ShapeDtypeStruct((rows, outs - DH), jnp.bfloat16),
        ],
        compiler_params=pltpu.CompilerParams(vmem_limit_bytes=48 * 1024 * 1024),
        cost_estimate=pl.CostEstimate(
            flops=2 * rows * width * outs + 10 * rows * width,
            transcendentals=rows,
            bytes_accessed=2 * rows * width + 2 * width * outs + 2 * rows * outs,
        ),
        input_output_aliases={3: 0, 4: 1},
    )(
        rows_t,
        mod_cols,
        weights_t,
        pltpu.with_memory_space_constraint(q_init, pltpu.HBM),
        pltpu.with_memory_space_constraint(kv_init, pltpu.HBM),
    )


def attention_kernel(q_ref, kv_ref, o_ref):
    keys = kv_ref[:, :DH]
    values = kv_ref[:, DH:]
    scores = lax.dot_general(
        q_ref[...], keys, (((1,), (1,)), ((), ())), preferred_element_type=jnp.float32
    ) * (DH ** (-0.5))
    shifted = jnp.exp(scores - jnp.max(scores, axis=1, keepdims=True))
    row_sum = jnp.sum(shifted, axis=1, keepdims=True)
    numer = jnp.dot(shifted.astype(jnp.bfloat16), values, preferred_element_type=jnp.float32)
    o_ref[...] = (numer / row_sum).astype(o_ref.dtype)


def attention(queries, key_values, block=256):
    rows = queries.shape[0]
    count = key_values.shape[0]
    return pl.pallas_call(
        attention_kernel,
        grid=(rows // block,),
        in_specs=[
            pl.BlockSpec((block, DH), lambda i: (i, 0)),
            pl.BlockSpec((count, 2 * DH), lambda i: (0, 0)),
        ],
        out_specs=pl.BlockSpec((block, DH), lambda i: (i, 0)),
        out_shape=jax.ShapeDtypeStruct((rows, DH), jnp.bfloat16),
        compiler_params=pltpu.CompilerParams(vmem_limit_bytes=56 * 1024 * 1024),
        cost_estimate=pl.CostEstimate(
            flops=4 * rows * count * DH,
            transcendentals=rows * count,
            bytes_accessed=4 * rows * DH + 4 * count * DH,
        ),
    )(queries, key_values)


def body(tokens, defect_mask, timestep, mask_embed, mod_weight, w_qkv, w_out):
    tok_rows = tokens.shape[0]
    residual_in = tokens + defect_mask.astype(jnp.bfloat16)[:, None] * mask_embed[None, :]
    tok_count = lax.axis_size("tok")
    w_copies = jnp.broadcast_to(w_qkv[None], (tok_count,) + w_qkv.shape)
    w_full = lax.all_to_all(w_copies, "tok", split_axis=0, concat_axis=0, tiled=True)
    w_full = w_full.reshape((tok_count * w_qkv.shape[0],) + w_qkv.shape[1:])
    half_width = TEMB // 2
    frequency = jnp.exp(-math.log(10000.0) * jnp.arange(half_width, dtype=jnp.float32) / half_width)
    angles = timestep.astype(jnp.float32)[0] * frequency
    embedding = jnp.concatenate([jnp.cos(angles), jnp.sin(angles)])
    modulation = jnp.einsum(
        "e,ecf->cf",
        jax.nn.silu(embedding),
        mod_weight.astype(jnp.float32),
        precision=lax.Precision.HIGHEST,
    ).astype(jnp.bfloat16)
    residual_full = lax.all_gather(residual_in, "wid", axis=1, tiled=True)
    wid_count = lax.axis_size("wid")
    mod_copies = jnp.broadcast_to(modulation[None, :2], (wid_count, 2, modulation.shape[1]))
    mod_parts = lax.all_to_all(mod_copies, "wid", split_axis=0, concat_axis=0, tiled=True)
    shift_scale = jnp.transpose(mod_parts, (1, 0, 2)).reshape(2, wid_count * modulation.shape[1])
    w_rows = w_full.reshape(w_full.shape[0], 3 * DH)[:tok_rows]
    q_init = w_rows[:, :DH]
    kv_init = w_rows[:, DH:]
    q_init, kv_init, w_full = lax.optimization_barrier((q_init, kv_init, w_full))
    weights_t = w_full.reshape(w_full.shape[0], 3 * DH).T
    qkv = tuple(project(residual_full.T, shift_scale.T, weights_t, q_init, kv_init))
    w_late, qkv = lax.optimization_barrier((w_out, qkv))
    w_cols = lax.all_to_all(w_late, "wid", split_axis=1, concat_axis=0, tiled=True)
    queries, key_rows = qkv
    key_values = lax.all_gather(key_rows, "tok", axis=0, tiled=True)
    w_cols, key_values = lax.optimization_barrier((w_cols, key_values))
    attended = attention(queries, key_values)
    heads = lax.all_gather(attended, "wid", axis=0, tiled=False)
    projected = jnp.einsum(
        "htd,hdc->tc",
        heads,
        w_cols.reshape(heads.shape[0], DH, w_cols.shape[1]),
        preferred_element_type=jnp.float32,
    )
    return (
        residual_in.astype(jnp.float32) + modulation[2].astype(jnp.float32)[None, :] * projected
    ).astype(jnp.bfloat16)


def solution(mesh):
    return jax.shard_map(
        body,
        mesh=mesh,
        in_specs=(
            P("tok", "wid"),
            P("tok"),
            P(),
            P("wid"),
            P(None, None, "wid"),
            P("tok", None, "wid"),
            P("wid", None),
        ),
        out_specs=P("tok", "wid"),
        check_vma=False,
    )
```

```python
import math

import jax
import jax.numpy as jnp
from jax import lax
from jax.experimental import pallas as pl
from jax.experimental.pallas import tpu as pltpu
from jax.sharding import PartitionSpec as P

D = 3072
DH = 128
TEMB = 256


def finish_rows(values, row_mean, row_var, shift_row, scale_row):
    normal = (values - row_mean) * lax.rsqrt(row_var + 1e-06)
    return (normal * (1.0 + scale_row.astype(jnp.float32)) + shift_row.astype(jnp.float32)).astype(
        jnp.bfloat16
    )


def project_kernel(x_ref, mod_ref, w_ref, q_init, kv_init, q_ref, kv_ref):
    values = x_ref[...].astype(jnp.float32)
    width = values.shape[0]
    row_mean = jnp.sum(values, axis=0, keepdims=True) / width
    row_var = jnp.sum(values * values, axis=0, keepdims=True) / width - row_mean * row_mean
    normal = (values - row_mean) * lax.rsqrt(row_var + 1e-06)
    shift_col = mod_ref[:, 0:1].astype(jnp.float32)
    scale_col = mod_ref[:, 1:2].astype(jnp.float32)
    normed = (normal * (1.0 + scale_col) + shift_col).astype(jnp.bfloat16)
    qkv_t = jnp.dot(w_ref[...], normed, preferred_element_type=jnp.float32)
    qkv = jnp.transpose(qkv_t).astype(jnp.bfloat16)
    q_ref[...] = qkv[:, :DH]
    kv_ref[...] = qkv[:, DH:]


def project(rows_t, mod_cols, weights_t, q_init, kv_init, block=512):
    width, rows = rows_t.shape
    outs = weights_t.shape[0]
    return pl.pallas_call(
        project_kernel,
        grid=(rows // block,),
        in_specs=[
            pl.BlockSpec((width, block), lambda i: (0, i)),
            pl.BlockSpec(mod_cols.shape, lambda i: (0, 0)),
            pl.BlockSpec(weights_t.shape, lambda i: (0, 0)),
            pl.BlockSpec(memory_space=pltpu.HBM),
            pl.BlockSpec(memory_space=pltpu.HBM),
        ],
        out_specs=[
            pl.BlockSpec((block, DH), lambda i: (i, 0)),
            pl.BlockSpec((block, outs - DH), lambda i: (i, 0)),
        ],
        out_shape=[
            jax.ShapeDtypeStruct((rows, DH), jnp.bfloat16),
            jax.ShapeDtypeStruct((rows, outs - DH), jnp.bfloat16),
        ],
        compiler_params=pltpu.CompilerParams(vmem_limit_bytes=48 * 1024 * 1024),
        cost_estimate=pl.CostEstimate(
            flops=2 * rows * width * outs + 10 * rows * width,
            transcendentals=rows,
            bytes_accessed=2 * rows * width + 2 * width * outs + 2 * rows * outs,
        ),
        input_output_aliases={3: 0, 4: 1},
    )(
        rows_t,
        mod_cols,
        weights_t,
        pltpu.with_memory_space_constraint(q_init, pltpu.HBM),
        pltpu.with_memory_space_constraint(kv_init, pltpu.HBM),
    )


def attention_kernel(q_ref, kv_ref, o_ref):
    keys = kv_ref[:, :DH]
    values = kv_ref[:, DH:]
    scores = lax.dot_general(
        q_ref[...], keys, (((1,), (1,)), ((), ())), preferred_element_type=jnp.float32
    ) * (DH ** (-0.5))
    shifted = jnp.exp(scores - jnp.max(scores, axis=1, keepdims=True))
    row_sum = jnp.sum(shifted, axis=1, keepdims=True)
    numer = jnp.dot(shifted.astype(jnp.bfloat16), values, preferred_element_type=jnp.float32)
    o_ref[...] = (numer / row_sum).astype(o_ref.dtype)


def attention(queries, key_values, block=256):
    rows = queries.shape[0]
    count = key_values.shape[0]
    return pl.pallas_call(
        attention_kernel,
        grid=(rows // block,),
        in_specs=[
            pl.BlockSpec((block, DH), lambda i: (i, 0)),
            pl.BlockSpec((count, 2 * DH), lambda i: (0, 0)),
        ],
        out_specs=pl.BlockSpec((block, DH), lambda i: (i, 0)),
        out_shape=jax.ShapeDtypeStruct((rows, DH), jnp.bfloat16),
        compiler_params=pltpu.CompilerParams(vmem_limit_bytes=56 * 1024 * 1024),
        cost_estimate=pl.CostEstimate(
            flops=4 * rows * count * DH,
            transcendentals=rows * count,
            bytes_accessed=4 * rows * DH + 4 * count * DH,
        ),
    )(queries, key_values)


def body(tokens, defect_mask, timestep, mask_embed, mod_weight, w_qkv, w_out):
    tok_rows = tokens.shape[0]
    residual_in = tokens + defect_mask.astype(jnp.bfloat16)[:, None] * mask_embed[None, :]
    tok_count = lax.axis_size("tok")
    w_copies = jnp.broadcast_to(w_qkv[None], (tok_count,) + w_qkv.shape)
    w_full = lax.all_to_all(w_copies, "tok", split_axis=0, concat_axis=0, tiled=True)
    w_full = w_full.reshape((tok_count * w_qkv.shape[0],) + w_qkv.shape[1:])
    half_width = TEMB // 2
    frequency = jnp.exp(-math.log(10000.0) * jnp.arange(half_width, dtype=jnp.float32) / half_width)
    angles = timestep.astype(jnp.float32)[0] * frequency
    embedding = jnp.concatenate([jnp.cos(angles), jnp.sin(angles)])
    modulation = jnp.einsum(
        "e,ecf->cf",
        jax.nn.silu(embedding),
        mod_weight.astype(jnp.float32),
        precision=lax.Precision.HIGHEST,
    ).astype(jnp.bfloat16)
    residual_full = lax.all_gather(residual_in, "wid", axis=1, tiled=True)
    wid_count = lax.axis_size("wid")
    mod_copies = jnp.broadcast_to(modulation[None, :2], (wid_count, 2, modulation.shape[1]))
    mod_parts = lax.all_to_all(mod_copies, "wid", split_axis=0, concat_axis=0, tiled=True)
    shift_scale = jnp.transpose(mod_parts, (1, 0, 2)).reshape(2, wid_count * modulation.shape[1])
    w_rows = w_full.reshape(w_full.shape[0], 3 * DH)[:tok_rows]
    q_init = w_rows[:, :DH]
    kv_init = w_rows[:, DH:]
    q_init, kv_init, w_full = lax.optimization_barrier((q_init, kv_init, w_full))
    weights_t = w_full.reshape(w_full.shape[0], 3 * DH).T
    qkv = tuple(project(residual_full.T, shift_scale.T, weights_t, q_init, kv_init))
    w_late, qkv = lax.optimization_barrier((w_out, qkv))
    w_cols = lax.all_to_all(w_late, "wid", split_axis=1, concat_axis=0, tiled=True)
    queries, key_rows = qkv
    key_values = lax.all_gather(key_rows, "tok", axis=0, tiled=True)
    w_cols, key_values = lax.optimization_barrier((w_cols, key_values))
    attended = attention(queries, key_values)
    heads = lax.all_gather(attended, "wid", axis=0, tiled=False)
    projected = jnp.einsum(
        "htd,hdc->tc",
        heads,
        w_cols.reshape(heads.shape[0], DH, w_cols.shape[1]),
        preferred_element_type=jnp.float32,
    )
    return (
        residual_in.astype(jnp.float32) + modulation[2].astype(jnp.float32)[None, :] * projected
    ).astype(jnp.bfloat16)


def solution(mesh):
    return jax.shard_map(
        body,
        mesh=mesh,
        in_specs=(
            P("tok", "wid"),
            P("tok"),
            P(),
            P("wid"),
            P(None, None, "wid"),
            P("tok", None, "wid"),
            P("wid", None),
        ),
        out_specs=P("tok", "wid"),
        check_vma=False,
    )
```

```python
import math

import jax
import jax.numpy as jnp
from jax import lax
from jax.experimental import pallas as pl
from jax.experimental.pallas import tpu as pltpu
from jax.sharding import PartitionSpec as P

D = 3072
DH = 128
TEMB = 256


def finish_rows(values, row_mean, row_var, shift_row, scale_row):
    normal = (values - row_mean) * lax.rsqrt(row_var + 1e-06)
    return (normal * (1.0 + scale_row.astype(jnp.float32)) + shift_row.astype(jnp.float32)).astype(
        jnp.bfloat16
    )


def project_kernel(x_ref, mod_ref, w_ref, q_init, kv_init, q_ref, kv_ref):
    rows = x_ref[...]
    values = rows.astype(jnp.float32)
    width = values.shape[0]
    ones = jnp.ones((8, width), jnp.bfloat16)
    row_mean = jnp.dot(ones, rows, preferred_element_type=jnp.float32)[0:1] / width
    row_var = jnp.sum(values * values, axis=0, keepdims=True) / width - row_mean * row_mean
    normal = (values - row_mean) * lax.rsqrt(row_var + 1e-06)
    shift_col = mod_ref[:, 0:1].astype(jnp.float32)
    scale_col = mod_ref[:, 1:2].astype(jnp.float32)
    normed = (normal * (1.0 + scale_col) + shift_col).astype(jnp.bfloat16)
    qkv_t = jnp.dot(w_ref[...], normed, preferred_element_type=jnp.float32)
    qkv = jnp.transpose(qkv_t).astype(jnp.bfloat16)
    q_ref[...] = qkv[:, :DH]
    kv_ref[...] = qkv[:, DH:]


def project(rows_t, mod_cols, weights_t, q_init, kv_init, block=512):
    width, rows = rows_t.shape
    outs = weights_t.shape[0]
    return pl.pallas_call(
        project_kernel,
        grid=(rows // block,),
        in_specs=[
            pl.BlockSpec((width, block), lambda i: (0, i)),
            pl.BlockSpec(mod_cols.shape, lambda i: (0, 0)),
            pl.BlockSpec(weights_t.shape, lambda i: (0, 0)),
            pl.BlockSpec(memory_space=pltpu.HBM),
            pl.BlockSpec(memory_space=pltpu.HBM),
        ],
        out_specs=[
            pl.BlockSpec((block, DH), lambda i: (i, 0)),
            pl.BlockSpec((block, outs - DH), lambda i: (i, 0)),
        ],
        out_shape=[
            jax.ShapeDtypeStruct((rows, DH), jnp.bfloat16),
            jax.ShapeDtypeStruct((rows, outs - DH), jnp.bfloat16),
        ],
        compiler_params=pltpu.CompilerParams(vmem_limit_bytes=48 * 1024 * 1024),
        cost_estimate=pl.CostEstimate(
            flops=2 * rows * width * outs + 10 * rows * width,
            transcendentals=rows,
            bytes_accessed=2 * rows * width + 2 * width * outs + 2 * rows * outs,
        ),
        input_output_aliases={3: 0, 4: 1},
    )(
        rows_t,
        mod_cols,
        weights_t,
        pltpu.with_memory_space_constraint(q_init, pltpu.HBM),
        pltpu.with_memory_space_constraint(kv_init, pltpu.HBM),
    )


def attention_kernel(q_ref, kv_ref, o_ref):
    keys = kv_ref[:, :DH]
    values = kv_ref[:, DH:]
    scores = lax.dot_general(
        q_ref[...], keys, (((1,), (1,)), ((), ())), preferred_element_type=jnp.float32
    ) * (DH ** (-0.5))
    shifted = jnp.exp(scores - jnp.max(scores, axis=1, keepdims=True))
    row_sum = jnp.sum(shifted, axis=1, keepdims=True)
    numer = jnp.dot(shifted.astype(jnp.bfloat16), values, preferred_element_type=jnp.float32)
    o_ref[...] = (numer / row_sum).astype(o_ref.dtype)


def attention(queries, key_values, block=256):
    rows = queries.shape[0]
    count = key_values.shape[0]
    return pl.pallas_call(
        attention_kernel,
        grid=(rows // block,),
        in_specs=[
            pl.BlockSpec((block, DH), lambda i: (i, 0)),
            pl.BlockSpec((count, 2 * DH), lambda i: (0, 0)),
        ],
        out_specs=pl.BlockSpec((block, DH), lambda i: (i, 0)),
        out_shape=jax.ShapeDtypeStruct((rows, DH), jnp.bfloat16),
        compiler_params=pltpu.CompilerParams(vmem_limit_bytes=56 * 1024 * 1024),
        cost_estimate=pl.CostEstimate(
            flops=4 * rows * count * DH,
            transcendentals=rows * count,
            bytes_accessed=4 * rows * DH + 4 * count * DH,
        ),
    )(queries, key_values)


def body(tokens, defect_mask, timestep, mask_embed, mod_weight, w_qkv, w_out):
    tok_rows = tokens.shape[0]
    residual_in = tokens + defect_mask.astype(jnp.bfloat16)[:, None] * mask_embed[None, :]
    tok_count = lax.axis_size("tok")
    w_copies = jnp.broadcast_to(w_qkv[None], (tok_count,) + w_qkv.shape)
    w_full = lax.all_to_all(w_copies, "tok", split_axis=0, concat_axis=0, tiled=True)
    w_full = w_full.reshape((tok_count * w_qkv.shape[0],) + w_qkv.shape[1:])
    half_width = TEMB // 2
    frequency = jnp.exp(-math.log(10000.0) * jnp.arange(half_width, dtype=jnp.float32) / half_width)
    angles = timestep.astype(jnp.float32)[0] * frequency
    embedding = jnp.concatenate([jnp.cos(angles), jnp.sin(angles)])
    modulation = jnp.einsum(
        "e,ecf->cf",
        jax.nn.silu(embedding),
        mod_weight.astype(jnp.float32),
        precision=lax.Precision.HIGHEST,
    ).astype(jnp.bfloat16)
    residual_full = lax.all_gather(residual_in, "wid", axis=1, tiled=True)
    wid_count = lax.axis_size("wid")
    mod_copies = jnp.broadcast_to(modulation[None, :2], (wid_count, 2, modulation.shape[1]))
    mod_parts = lax.all_to_all(mod_copies, "wid", split_axis=0, concat_axis=0, tiled=True)
    shift_scale = jnp.transpose(mod_parts, (1, 0, 2)).reshape(2, wid_count * modulation.shape[1])
    w_rows = w_full.reshape(w_full.shape[0], 3 * DH)[:tok_rows]
    q_init = w_rows[:, :DH]
    kv_init = w_rows[:, DH:]
    q_init, kv_init, w_full = lax.optimization_barrier((q_init, kv_init, w_full))
    weights_t = w_full.reshape(w_full.shape[0], 3 * DH).T
    qkv = tuple(project(residual_full.T, shift_scale.T, weights_t, q_init, kv_init))
    w_late, qkv = lax.optimization_barrier((w_out, qkv))
    w_cols = lax.all_to_all(w_late, "wid", split_axis=1, concat_axis=0, tiled=True)
    queries, key_rows = qkv
    key_values = lax.all_gather(key_rows, "tok", axis=0, tiled=True)
    w_cols, key_values = lax.optimization_barrier((w_cols, key_values))
    attended = attention(queries, key_values)
    heads = lax.all_gather(attended, "wid", axis=0, tiled=False)
    projected = jnp.einsum(
        "htd,hdc->tc",
        heads,
        w_cols.reshape(heads.shape[0], DH, w_cols.shape[1]),
        preferred_element_type=jnp.float32,
    )
    return (
        residual_in.astype(jnp.float32) + modulation[2].astype(jnp.float32)[None, :] * projected
    ).astype(jnp.bfloat16)


def solution(mesh):
    return jax.shard_map(
        body,
        mesh=mesh,
        in_specs=(
            P("tok", "wid"),
            P("tok"),
            P(),
            P("wid"),
            P(None, None, "wid"),
            P("tok", None, "wid"),
            P("wid", None),
        ),
        out_specs=P("tok", "wid"),
        check_vma=False,
    )
```

```python
import math

import jax
import jax.numpy as jnp
from jax import lax
from jax.experimental import pallas as pl
from jax.experimental.pallas import tpu as pltpu
from jax.sharding import PartitionSpec as P

D = 3072
DH = 128
TEMB = 256


def finish_rows(values, row_mean, row_var, shift_row, scale_row):
    normal = (values - row_mean) * lax.rsqrt(row_var + 1e-06)
    return (normal * (1.0 + scale_row.astype(jnp.float32)) + shift_row.astype(jnp.float32)).astype(
        jnp.bfloat16
    )


def project_kernel(x_ref, mod_ref, w_ref, q_init, kv_init, q_ref, kv_ref):
    rows = x_ref[...]
    values = rows.astype(jnp.float32)
    width = values.shape[0]
    ones = jnp.ones((8, width), jnp.bfloat16)
    row_mean = jnp.dot(ones, rows, preferred_element_type=jnp.float32)[0:1] / width
    row_var = jnp.sum(values * values, axis=0, keepdims=True) / width - row_mean * row_mean
    normal = (values - row_mean) * lax.rsqrt(row_var + 1e-06)
    shift_col = mod_ref[:, 0:1].astype(jnp.float32)
    scale_col = mod_ref[:, 1:2].astype(jnp.float32)
    normed = (normal * (1.0 + scale_col) + shift_col).astype(jnp.bfloat16)
    qkv_t = jnp.dot(w_ref[...], normed, preferred_element_type=jnp.float32)
    qkv = jnp.transpose(qkv_t.astype(jnp.bfloat16))
    q_ref[...] = qkv[:, :DH]
    kv_ref[...] = qkv[:, DH:]


def project(rows_t, mod_cols, weights_t, q_init, kv_init, block=512):
    width, rows = rows_t.shape
    outs = weights_t.shape[0]
    return pl.pallas_call(
        project_kernel,
        grid=(rows // block,),
        in_specs=[
            pl.BlockSpec((width, block), lambda i: (0, i)),
            pl.BlockSpec(mod_cols.shape, lambda i: (0, 0)),
            pl.BlockSpec(weights_t.shape, lambda i: (0, 0)),
            pl.BlockSpec(memory_space=pltpu.HBM),
            pl.BlockSpec(memory_space=pltpu.HBM),
        ],
        out_specs=[
            pl.BlockSpec((block, DH), lambda i: (i, 0)),
            pl.BlockSpec((block, outs - DH), lambda i: (i, 0)),
        ],
        out_shape=[
            jax.ShapeDtypeStruct((rows, DH), jnp.bfloat16),
            jax.ShapeDtypeStruct((rows, outs - DH), jnp.bfloat16),
        ],
        compiler_params=pltpu.CompilerParams(vmem_limit_bytes=48 * 1024 * 1024),
        cost_estimate=pl.CostEstimate(
            flops=2 * rows * width * outs + 10 * rows * width,
            transcendentals=rows,
            bytes_accessed=2 * rows * width + 2 * width * outs + 2 * rows * outs,
        ),
        input_output_aliases={3: 0, 4: 1},
    )(
        rows_t,
        mod_cols,
        weights_t,
        pltpu.with_memory_space_constraint(q_init, pltpu.HBM),
        pltpu.with_memory_space_constraint(kv_init, pltpu.HBM),
    )


def attention_kernel(q_ref, kv_ref, o_ref):
    keys = kv_ref[:, :DH]
    values = kv_ref[:, DH:]
    scores = lax.dot_general(
        q_ref[...], keys, (((1,), (1,)), ((), ())), preferred_element_type=jnp.float32
    ) * (DH ** (-0.5))
    shifted = jnp.exp(scores - jnp.max(scores, axis=1, keepdims=True))
    row_sum = jnp.sum(shifted, axis=1, keepdims=True)
    numer = jnp.dot(shifted.astype(jnp.bfloat16), values, preferred_element_type=jnp.float32)
    o_ref[...] = (numer / row_sum).astype(o_ref.dtype)


def attention(queries, key_values, block=256):
    rows = queries.shape[0]
    count = key_values.shape[0]
    return pl.pallas_call(
        attention_kernel,
        grid=(rows // block,),
        in_specs=[
            pl.BlockSpec((block, DH), lambda i: (i, 0)),
            pl.BlockSpec((count, 2 * DH), lambda i: (0, 0)),
        ],
        out_specs=pl.BlockSpec((block, DH), lambda i: (i, 0)),
        out_shape=jax.ShapeDtypeStruct((rows, DH), jnp.bfloat16),
        compiler_params=pltpu.CompilerParams(vmem_limit_bytes=56 * 1024 * 1024),
        cost_estimate=pl.CostEstimate(
            flops=4 * rows * count * DH,
            transcendentals=rows * count,
            bytes_accessed=4 * rows * DH + 4 * count * DH,
        ),
    )(queries, key_values)


def body(tokens, defect_mask, timestep, mask_embed, mod_weight, w_qkv, w_out):
    tok_rows = tokens.shape[0]
    residual_in = tokens + defect_mask.astype(jnp.bfloat16)[:, None] * mask_embed[None, :]
    tok_count = lax.axis_size("tok")
    w_copies = jnp.broadcast_to(w_qkv[None], (tok_count,) + w_qkv.shape)
    w_full = lax.all_to_all(w_copies, "tok", split_axis=0, concat_axis=0, tiled=True)
    w_full = w_full.reshape((tok_count * w_qkv.shape[0],) + w_qkv.shape[1:])
    half_width = TEMB // 2
    frequency = jnp.exp(-math.log(10000.0) * jnp.arange(half_width, dtype=jnp.float32) / half_width)
    angles = timestep.astype(jnp.float32)[0] * frequency
    embedding = jnp.concatenate([jnp.cos(angles), jnp.sin(angles)])
    modulation = jnp.einsum(
        "e,ecf->cf",
        jax.nn.silu(embedding),
        mod_weight.astype(jnp.float32),
        precision=lax.Precision.HIGHEST,
    ).astype(jnp.bfloat16)
    residual_full = lax.all_gather(residual_in, "wid", axis=1, tiled=True)
    wid_count = lax.axis_size("wid")
    mod_copies = jnp.broadcast_to(modulation[None, :2], (wid_count, 2, modulation.shape[1]))
    mod_parts = lax.all_to_all(mod_copies, "wid", split_axis=0, concat_axis=0, tiled=True)
    shift_scale = jnp.transpose(mod_parts, (1, 0, 2)).reshape(2, wid_count * modulation.shape[1])
    w_rows = w_full.reshape(w_full.shape[0], 3 * DH)[:tok_rows]
    q_init = w_rows[:, :DH]
    kv_init = w_rows[:, DH:]
    q_init, kv_init, w_full = lax.optimization_barrier((q_init, kv_init, w_full))
    weights_t = w_full.reshape(w_full.shape[0], 3 * DH).T
    qkv = tuple(project(residual_full.T, shift_scale.T, weights_t, q_init, kv_init))
    w_late, qkv = lax.optimization_barrier((w_out, qkv))
    w_cols = lax.all_to_all(w_late, "wid", split_axis=1, concat_axis=0, tiled=True)
    queries, key_rows = qkv
    key_values = lax.all_gather(key_rows, "tok", axis=0, tiled=True)
    w_cols, key_values = lax.optimization_barrier((w_cols, key_values))
    attended = attention(queries, key_values)
    heads = lax.all_gather(attended, "wid", axis=0, tiled=False)
    projected = jnp.einsum(
        "htd,hdc->tc",
        heads,
        w_cols.reshape(heads.shape[0], DH, w_cols.shape[1]),
        preferred_element_type=jnp.float32,
    )
    return (
        residual_in.astype(jnp.float32) + modulation[2].astype(jnp.float32)[None, :] * projected
    ).astype(jnp.bfloat16)


def solution(mesh):
    return jax.shard_map(
        body,
        mesh=mesh,
        in_specs=(
            P("tok", "wid"),
            P("tok"),
            P(),
            P("wid"),
            P(None, None, "wid"),
            P("tok", None, "wid"),
            P("wid", None),
        ),
        out_specs=P("tok", "wid"),
        check_vma=False,
    )
```
